32 devices in a mesh: groups: 2 (over x), visit: 8 (over z, y), tile: 2 (over core).
Axes of the slice: x: 2, y: 2, z: 4, core: 2. Of those that a mesh axis runs over, the one named last changes fastest.
Arguments:
- exposure: float32 [16, 512, 2048], P(('groups', 'visit'), 'tile'), parts along dimension 0, may hold values from -12 to 12, as said below
- partners: int32 [16, 8], P('groups'), parts along dimension 0, may hold values from 0 to 7, as said below
- offsets: int32 [16, 8], P('groups'), parts along dimension 0, may hold values from -32 to 32
- stamps: int32 [16, 2, 8, 2], P(('groups', 'visit'), 'tile'), parts along dimension 0, may hold values from 0 to 1920, as said below
Outputs:
- difference: float32 [16, 512, 2048], P(('groups', 'visit'), 'tile'), parts along dimension 0
- coefficients: float32 [16, 33], P(('groups', 'visit')), parts along dimension 0
The draws below stay inside these ranges and needn't reach their ends.
There are 2 independent parts, one for each index of `groups`. The reference program is written for one: setup_inputs(seed, part) draws one part's arguments, and reference() takes and returns one part's arrays. A program takes and returns all parts, laid end to end along the dimension named above; each array names one. Nothing has to cross between parts.
Inputs may be any that keep to these rules, and one draw needn't show every extreme that they name: Every row of partners names each of the 8 visits once, and so does every column. `stamps`: A stamp's row anchor lies in 0..128, its column anchor in 0..1920. `exposure`: images of order one.
All inputs are finite; a program needn't handle non-finite values.
Results may differ from the reference program's by a relative error of at most 0.0003.
Values sent between devices are 32-bit elements; how exact they have to be, the bound alone decides.
No kernel may reach another device: no remote copies, remote signals or barrier semaphores. Data moves between devices by JAX's collectives and lax.ppermute only.
A program may use at most 128 MiB of HBM per device.

```python
import jax
import jax.numpy as jnp
from jax import lax

ROWS = 256
COLS = 2048
NSTAMP = 8
STAMP = 128
KERNEL = 31
TERMS = 11
SHIFT = 32
VISITS = 8
TILES = 2
HEIGHT = 512
BLOCK = 32


def partner_tables(key):
    first = jax.random.permutation(jax.random.fold_in(key, 11), VISITS)
    second = jax.random.permutation(jax.random.fold_in(key, 12), VISITS)
    sources = (first[:, None] + second[None, :]) % VISITS
    pointing = jax.random.randint(jax.random.fold_in(key, 13), (VISITS,), 0, SHIFT + 1)
    order = jax.random.permutation(jax.random.fold_in(key, 14), VISITS)
    pointing = pointing.at[order[0]].set(0).at[order[1]].set(SHIFT)
    amounts = pointing[:, None] - pointing[sources]
    return (sources.astype(jnp.int32), pointing.astype(jnp.int32), amounts.astype(jnp.int32))


def draw_partners(key, part):
    return partner_tables(key)[0]


def draw_offsets(key, part):
    return partner_tables(key)[2]


def draw_exposure(key, part):
    sources, pointing, amounts = partner_tables(key)
    shape_sky = (HEIGHT, COLS + SHIFT)
    shape_all = (VISITS, HEIGHT, COLS)
    sky = jnp.clip(jax.random.normal(jax.random.fold_in(key, 21), shape_sky, jnp.float32), -5.0, 5.0)
    noise = 0.3 * jnp.clip(jax.random.normal(jax.random.fold_in(key, 22), shape_all, jnp.float32), -4.0, 4.0)
    level = jnp.exp(jax.random.uniform(jax.random.fold_in(key, 23), (VISITS,), jnp.float32, jnp.log(0.7), jnp.log(1.4)))
    curve = jax.random.uniform(jax.random.fold_in(key, 24), (VISITS,), jnp.float32, -0.4, 0.4)
    background = jax.random.uniform(jax.random.fold_in(key, 25), (VISITS,), jnp.float32, -0.5, 0.5)
    slope = jax.random.uniform(jax.random.fold_in(key, 26), (VISITS,), jnp.float32, -0.3, 0.3)
    row_coord = (2.0 * jnp.arange(HEIGHT).astype(jnp.float32) + 1.0) / HEIGHT - 1.0
    col_coord = (2.0 * jnp.arange(COLS).astype(jnp.float32) + 1.0) / COLS - 1.0

    def drawn_sky(amount):
        return lax.dynamic_slice_in_dim(sky, amount, COLS, 1)
    aligned = jax.vmap(drawn_sky)(pointing)
    gain = level[:, None, None] * (1.0 + curve[:, None, None] * row_coord[None, :, None] ** 2)
    return gain * aligned + noise + background[:, None, None] + slope[:, None, None] * col_coord[None, None, :]


def draw_stamps(key, part):
    rows = jax.random.randint(jax.random.fold_in(key, 31), (VISITS, TILES, NSTAMP), 0, ROWS - STAMP + 1)
    cols = jax.random.randint(jax.random.fold_in(key, 32), (VISITS, TILES, NSTAMP), 0, COLS - STAMP + 1)
    rows = rows.at[0, 0, 0].set(ROWS - STAMP).at[0, 0, 1].set(0)
    cols = cols.at[0, 0, 0].set(COLS - STAMP).at[0, 0, 1].set(0)
    return jnp.stack([rows, cols], axis=-1).astype(jnp.int32)


def setup_inputs(seed: int = 0, part: int = 0) -> dict:
    splits = jax.random.split(jax.random.key(seed), 5)
    own_keys = jax.random.split(jax.random.fold_in(splits[4], part), 5)
    exposure = draw_exposure(jax.random.fold_in(jax.random.fold_in(splits[4], part), 71), part)
    partners = draw_partners(jax.random.fold_in(jax.random.fold_in(splits[4], part), 71), part)
    offsets = draw_offsets(jax.random.fold_in(jax.random.fold_in(splits[4], part), 71), part)
    stamps = draw_stamps(jax.random.fold_in(jax.random.fold_in(splits[4], part), 71), part)
    return {"exposure": exposure, "partners": partners, "offsets": offsets, "stamps": stamps}


RIDGE = 0.05
SIGMA_LIST = (1.0, 1.0, 1.0, 2.0, 2.0, 4.0)
POWER_LIST = (0, 1, 2, 0, 1, 0)
COLUMN_PICK = (0, 1, 0, 2, 1, 0, 3, 4, 3, 5)
ROW_PICK = (0, 0, 1, 0, 1, 2, 3, 3, 4, 5)

def profiles():
    taps = (jnp.arange(KERNEL) - KERNEL // 2).astype(jnp.float32)
    stacked = []
    for sigma, power in zip(SIGMA_LIST, POWER_LIST):
        bell = jnp.exp(-taps * taps / (2.0 * sigma * sigma))
        stacked.append(bell * (taps / sigma) ** power / jnp.sum(bell))
    return jnp.stack(stacked)

def coordinates(count, first, total):
    return (2.0 * (first + jnp.arange(count)).astype(jnp.float32) + 1.0) / total - 1.0

def convolve_full(template, table):
    half = KERNEL // 2
    padded = jnp.pad(template, half)
    height = template.shape[0]
    width = template.shape[1]
    filtered = []
    for filter_index in range(6):
        total = jnp.zeros((height + 2 * half, width), jnp.float32)
        for offset_index in range(KERNEL):
            total = total + table[filter_index, offset_index] * padded[:, offset_index:offset_index + width]
        filtered.append(total)
    images = []
    for basis_index in range(10):
        source = filtered[COLUMN_PICK[basis_index]]
        total = jnp.zeros((height, width), jnp.float32)
        for offset_index in range(KERNEL):
            total = total + table[ROW_PICK[basis_index], offset_index] * source[offset_index:offset_index + height]
        images.append(total)
    return jnp.stack(images)

def design_sums(images, science, row_coord, col_coord):
    ones = jnp.ones((row_coord.shape[0], col_coord.shape[0]), jnp.float32)
    poly = jnp.stack([ones, ones * col_coord[None, :], ones * row_coord[:, None]])
    terms = (images[:, None] * poly[None]).reshape(30, -1)
    design = jnp.concatenate([terms, poly.reshape(3, -1)], axis=0)
    gram = jnp.dot(design, design.T, precision=lax.Precision.HIGHEST)
    vector = jnp.dot(design, science.reshape(-1), precision=lax.Precision.HIGHEST)
    return (gram, vector)

def solve_fit(gram, vector):
    regular = gram + RIDGE * jnp.diag(jnp.diag(gram))
    lower = jnp.linalg.cholesky(regular)
    return jax.scipy.linalg.cho_solve((lower, True), vector)

def model_of(images, solution, row_coord, col_coord):
    weights = solution[:30].reshape(10, 3)
    scale = weights[:, 0, None, None] + weights[:, 1, None, None] * col_coord[None, None, :] + weights[:, 2, None, None] * row_coord[None, :, None]
    background = solution[30] + solution[31] * col_coord[None, :] + solution[32] * row_coord[:, None]
    return jnp.sum(images * scale, axis=0) + background

def reference(exposure, partners, offsets, stamps):
    table = profiles()
    shifted_all = jnp.pad(exposure, ((0, 0), (0, 0), (SHIFT, SHIFT)))
    row_coord = coordinates(HEIGHT, 0, HEIGHT)
    col_coord = coordinates(COLS, 0, COLS)
    row_ids = jnp.arange(HEIGHT).astype(jnp.int32)
    block_ids = (row_ids % ROWS // BLOCK).astype(jnp.int32)
    zero_index = jnp.zeros((), jnp.int32)

    def pick_row(source, row_index, amount):
        start_col = (amount + SHIFT).astype(jnp.int32)
        return lax.dynamic_slice_in_dim(shifted_all[source, row_index], start_col, COLS)

    def one_visit(visit):
        sources = partners[visit][block_ids].astype(jnp.int32)
        amounts = offsets[visit][block_ids].astype(jnp.int32)
        template = jax.vmap(pick_row)(sources, row_ids, amounts)
        science = exposure[visit]
        images = convolve_full(template, table)
        tile_rows = (ROWS * jnp.arange(TILES)).astype(jnp.int32)
        anchor_rows = (stamps[visit][:, :, 0].astype(jnp.int32) + tile_rows[:, None]).reshape(-1)
        anchor_cols = stamps[visit][:, :, 1].astype(jnp.int32).reshape(-1)
        anchors = jnp.stack([anchor_rows, anchor_cols], axis=1).astype(jnp.int32)

        def add_stamp(carry, anchor):
            row_start = anchor[0].astype(jnp.int32)
            col_start = anchor[1].astype(jnp.int32)
            cut = lax.dynamic_slice(images, (zero_index, row_start, col_start), (10, STAMP, STAMP))
            science_cut = lax.dynamic_slice(science, (row_start, col_start), (STAMP, STAMP))
            row_part = lax.dynamic_slice_in_dim(row_coord, row_start, STAMP)
            col_part = lax.dynamic_slice_in_dim(col_coord, col_start, STAMP)
            gram_term, vector_term = design_sums(cut, science_cut, row_part, col_part)
            return ((carry[0] + gram_term, carry[1] + vector_term), None)
        start = (jnp.zeros((3 * TERMS, 3 * TERMS), jnp.float32), jnp.zeros((3 * TERMS,), jnp.float32))
        (gram, vector), _ = lax.scan(add_stamp, start, anchors)
        solution = solve_fit(gram, vector)
        return (science - model_of(images, solution, row_coord, col_coord), solution)
    difference, coefficients = lax.map(one_visit, jnp.arange(VISITS).astype(jnp.int32))
    return (difference, coefficients)
```

```python
import numpy as np
import jax
import jax.numpy as jnp
from jax import lax
from jax.sharding import PartitionSpec as P

STAMP = 128
KERNEL = 31
HALF = KERNEL // 2
TERMS = 11
SHIFT = 32
LANE = 128
HI = lax.Precision.HIGHEST


RIDGE = 0.05
SIGMA_LIST = (1.0, 1.0, 1.0, 2.0, 2.0, 4.0)
POWER_LIST = (0, 1, 2, 0, 1, 0)
COLUMN_PICK = (0, 1, 0, 2, 1, 0, 3, 4, 3, 5)
ROW_PICK = (0, 0, 1, 0, 1, 2, 3, 3, 4, 5)


def profile_table():
    taps = np.arange(KERNEL, dtype=np.float64) - HALF
    stacked = []
    for sigma, power in zip(SIGMA_LIST, POWER_LIST):
        bell = np.exp(-taps * taps / (2.0 * sigma * sigma))
        stacked.append(bell * (taps / sigma) ** power / np.sum(bell))
    return np.stack(stacked)


def column_bands(table):
    spans = np.arange(2 * LANE)[:, None] - np.arange(LANE)[None, :]
    inside = (spans >= 0) & (spans < KERNEL)
    picked = table[:, np.clip(spans, 0, KERNEL - 1)]
    return np.where(inside[None], picked, 0.0).astype(np.float32)


def row_bands(table, height):
    spans = np.arange(height + 2 * HALF)[None, :] - np.arange(height)[:, None]
    inside = (spans >= 0) & (spans < KERNEL)
    picked = table[:, np.clip(spans, 0, KERNEL - 1)]
    return np.where(inside[None], picked, 0.0).astype(np.float32)


def coordinates(count, first, total):
    return (
        2.0 * (first + jnp.arange(count, dtype=jnp.int32)).astype(jnp.float32) + 1.0
    ) / total - 1.0


def solve_fit(gram, vector):
    regular = gram + RIDGE * jnp.diag(jnp.diag(gram))
    lower = jnp.linalg.cholesky(regular)
    return jax.scipy.linalg.cho_solve((lower, True), vector)


def shards(exposure, partners, offsets, stamps):
    visits = lax.axis_size("visit")
    tiles = lax.axis_size("tile")
    me = lax.axis_index("visit")
    my_tile = lax.axis_index("tile")
    image = exposure[0]
    height, width = image.shape
    block = height // visits
    chunks = -(-(width + 2 * HALF) // LANE)
    padded_width = chunks * LANE
    table = profile_table()

    blocks = image.reshape(visits, block, width)
    dest_rows = jnp.argmax(partners == me, axis=1).astype(jnp.int32)
    send = jnp.concatenate(
        [lax.dynamic_index_in_dim(blocks, dest_rows[v], 0, keepdims=True) for v in range(visits)]
    )
    recv = lax.all_to_all(send, "visit", 0, 0, tiled=True)

    left = HALF + SHIFT
    right = 2 * SHIFT + padded_width - left - width
    recv_p = jnp.pad(recv, ((0, 0), (0, 0), (left, right)))
    my_sources = partners[me]
    my_amounts = offsets[me]
    pieces = [
        lax.dynamic_slice(
            recv_p, (my_sources[r], 0, SHIFT + my_amounts[r]), (1, block, padded_width)
        )[0]
        for r in range(visits)
    ]
    columns = jnp.arange(padded_width, dtype=jnp.int32)
    keep = (columns >= HALF) & (columns < HALF + width)
    placed = jnp.where(keep[None, :], jnp.concatenate(pieces, axis=0), 0.0)

    forward = [(i, i + 1) for i in range(tiles - 1)]
    backward = [(i + 1, i) for i in range(tiles - 1)]
    above = lax.ppermute(placed[height - HALF :], "tile", forward)
    below = lax.ppermute(placed[:HALF], "tile", backward)
    field = jnp.concatenate([above, placed, below], axis=0)
    field_rows = height + 2 * HALF

    tiled = field.reshape(field_rows, chunks, LANE)
    windows = jnp.concatenate([tiled[:, : chunks - 1], tiled[:, 1:]], axis=-1)
    col_band = jnp.asarray(column_bands(table))
    filtered = [
        jnp.einsum("ybk,kx->ybx", windows, col_band[f], precision=HI).reshape(
            field_rows, (chunks - 1) * LANE
        )[:, :width]
        for f in range(len(SIGMA_LIST))
    ]

    row_band = jnp.asarray(row_bands(table, height))
    images = jnp.stack(
        [
            jnp.dot(row_band[ROW_PICK[k]], filtered[COLUMN_PICK[k]], precision=HI)
            for k in range(len(COLUMN_PICK))
        ]
    )
    nimg = images.shape[0]

    row_coord = coordinates(height, my_tile * height, height * tiles)
    col_coord = coordinates(width, 0, width)

    anchors = stamps[0, 0]
    nstamp = anchors.shape[0]
    cuts, science, stamp_rows, stamp_cols = [], [], [], []
    for s in range(nstamp):
        row_start = anchors[s, 0]
        col_start = anchors[s, 1]
        cuts.append(lax.dynamic_slice(images, (0, row_start, col_start), (nimg, STAMP, STAMP)))
        science.append(lax.dynamic_slice(image, (row_start, col_start), (STAMP, STAMP)))
        stamp_rows.append(lax.dynamic_slice_in_dim(row_coord, row_start, STAMP))
        stamp_cols.append(lax.dynamic_slice_in_dim(col_coord, col_start, STAMP))
    cut = jnp.stack(cuts)
    science = jnp.stack(science).reshape(nstamp, STAMP * STAMP)
    ry = jnp.stack(stamp_rows)[:, :, None]
    cx = jnp.stack(stamp_cols)[:, None, :]
    ones = jnp.ones((nstamp, STAMP, STAMP), jnp.float32)
    poly = jnp.stack([ones, ones * cx, ones * ry], axis=1)
    terms = (cut[:, :, None] * poly[:, None]).reshape(nstamp, 3 * nimg, STAMP * STAMP)
    design = jnp.concatenate([terms, poly.reshape(nstamp, 3, STAMP * STAMP)], axis=1)
    gram = jnp.einsum("sip,sjp->ij", design, design, precision=HI)
    vector = jnp.einsum("sip,sp->i", design, science, precision=HI)
    gram, vector = lax.psum((gram, vector), "tile")
    solution = solve_fit(gram, vector)

    weights = solution[: 3 * nimg].reshape(nimg, 3)
    cxf = col_coord[None, :]
    ryf = row_coord[:, None]
    model = solution[3 * nimg] + solution[3 * nimg + 1] * cxf + solution[3 * nimg + 2] * ryf
    for k in range(nimg):
        model = model + images[k] * (weights[k, 0] + weights[k, 1] * cxf + weights[k, 2] * ryf)
    difference = image - model
    return (difference[None], solution[None])


def solution(mesh):
    return jax.shard_map(
        shards,
        mesh=mesh,
        in_specs=(
            P(("groups", "visit"), "tile", None),
            P("groups", None),
            P("groups", None),
            P(("groups", "visit"), "tile", None, None),
        ),
        out_specs=(P(("groups", "visit"), "tile", None), P(("groups", "visit"), None)),
        check_vma=False,
    )
```

```python
import numpy as np
import jax
import jax.numpy as jnp
from jax import lax
from jax.sharding import PartitionSpec as P

STAMP = 128
KERNEL = 31
HALF = KERNEL // 2
TERMS = 11
SHIFT = 32
LANE = 128
HI = lax.Precision.HIGHEST
CONV = lax.Precision.HIGH


RIDGE = 0.05
SIGMA_LIST = (1.0, 1.0, 1.0, 2.0, 2.0, 4.0)
POWER_LIST = (0, 1, 2, 0, 1, 0)
COLUMN_PICK = (0, 1, 0, 2, 1, 0, 3, 4, 3, 5)
ROW_PICK = (0, 0, 1, 0, 1, 2, 3, 3, 4, 5)


def profile_table():
    taps = np.arange(KERNEL, dtype=np.float64) - HALF
    stacked = []
    for sigma, power in zip(SIGMA_LIST, POWER_LIST):
        bell = np.exp(-taps * taps / (2.0 * sigma * sigma))
        stacked.append(bell * (taps / sigma) ** power / np.sum(bell))
    return np.stack(stacked)


def column_bands(table):
    spans = np.arange(2 * LANE)[:, None] - np.arange(LANE)[None, :]
    inside = (spans >= 0) & (spans < KERNEL)
    picked = table[:, np.clip(spans, 0, KERNEL - 1)]
    return np.where(inside[None], picked, 0.0).astype(np.float32)


def row_bands(table, height):
    spans = np.arange(height + 2 * HALF)[None, :] - np.arange(height)[:, None]
    inside = (spans >= 0) & (spans < KERNEL)
    picked = table[:, np.clip(spans, 0, KERNEL - 1)]
    return np.where(inside[None], picked, 0.0).astype(np.float32)


def coordinates(count, first, total):
    return (
        2.0 * (first + jnp.arange(count, dtype=jnp.int32)).astype(jnp.float32) + 1.0
    ) / total - 1.0


def solve_fit(gram, vector):
    regular = gram + RIDGE * jnp.diag(jnp.diag(gram))
    lower = jnp.linalg.cholesky(regular)
    return jax.scipy.linalg.cho_solve((lower, True), vector)


def shards(exposure, partners, offsets, stamps):
    visits = lax.axis_size("visit")
    tiles = lax.axis_size("tile")
    me = lax.axis_index("visit")
    my_tile = lax.axis_index("tile")
    image = exposure[0]
    height, width = image.shape
    block = height // visits
    chunks = -(-(width + 2 * HALF) // LANE)
    padded_width = chunks * LANE
    table = profile_table()

    blocks = image.reshape(visits, block, width)
    dest_rows = jnp.argmax(partners == me, axis=1).astype(jnp.int32)
    arrived = []
    for step in range(visits):
        target = (me + step) % visits
        piece = lax.dynamic_index_in_dim(blocks, dest_rows[target], 0, keepdims=True)
        if step:
            pairs = [(u, (u + step) % visits) for u in range(visits)]
            piece = lax.ppermute(piece, "visit", pairs)
        arrived.append(piece)
    recv = jnp.concatenate(arrived, axis=0)

    left = HALF + SHIFT
    right = 2 * SHIFT + padded_width - left - width
    recv_p = jnp.pad(recv, ((0, 0), (0, 0), (left, right)))
    my_steps = (me - partners[me]) % visits
    my_amounts = offsets[me]
    pieces = [
        lax.dynamic_slice(
            recv_p, (my_steps[r], 0, SHIFT + my_amounts[r]), (1, block, padded_width)
        )[0]
        for r in range(visits)
    ]
    columns = jnp.arange(padded_width, dtype=jnp.int32)
    keep = (columns >= HALF) & (columns < HALF + width)
    placed = jnp.where(keep[None, :], jnp.concatenate(pieces, axis=0), 0.0)

    forward = [(i, i + 1) for i in range(tiles - 1)]
    backward = [(i + 1, i) for i in range(tiles - 1)]
    above = lax.ppermute(placed[height - HALF :], "tile", forward)
    below = lax.ppermute(placed[:HALF], "tile", backward)
    field = jnp.concatenate([above, placed, below], axis=0)
    field_rows = height + 2 * HALF

    tiled = field.reshape(field_rows, chunks, LANE)
    windows = jnp.concatenate([tiled[:, : chunks - 1], tiled[:, 1:]], axis=-1)
    col_band = jnp.asarray(column_bands(table))
    filtered = [
        jnp.einsum("ybk,kx->ybx", windows, col_band[f], precision=CONV).reshape(
            field_rows, (chunks - 1) * LANE
        )[:, :width]
        for f in range(len(SIGMA_LIST))
    ]

    row_band = row_bands(table, height)
    found = {}
    for f in range(len(SIGMA_LIST)):
        terms = [k for k in range(len(COLUMN_PICK)) if COLUMN_PICK[k] == f]
        stacked_band = jnp.asarray(np.concatenate([row_band[ROW_PICK[k]] for k in terms]))
        out = jnp.dot(stacked_band, filtered[f], precision=CONV)
        for slot, k in enumerate(terms):
            found[k] = out[slot * height : (slot + 1) * height]
    images = jnp.stack([found[k] for k in range(len(COLUMN_PICK))])
    nimg = images.shape[0]

    row_coord = coordinates(height, my_tile * height, height * tiles)
    col_coord = coordinates(width, 0, width)

    anchors = stamps[0, 0]
    nstamp = anchors.shape[0]
    cuts, science, stamp_rows, stamp_cols = [], [], [], []
    for s in range(nstamp):
        row_start = anchors[s, 0]
        col_start = anchors[s, 1]
        cuts.append(lax.dynamic_slice(images, (0, row_start, col_start), (nimg, STAMP, STAMP)))
        science.append(lax.dynamic_slice(image, (row_start, col_start), (STAMP, STAMP)))
        stamp_rows.append(lax.dynamic_slice_in_dim(row_coord, row_start, STAMP))
        stamp_cols.append(lax.dynamic_slice_in_dim(col_coord, col_start, STAMP))
    pixels = nstamp * STAMP * STAMP
    cut = jnp.stack(cuts, axis=1).reshape(nimg, pixels)
    science = jnp.stack(science).reshape(1, pixels)
    ry = jnp.stack(stamp_rows)[:, :, None]
    cx = jnp.stack(stamp_cols)[:, None, :]
    ones = jnp.ones((nstamp, STAMP, STAMP), jnp.float32)
    poly = jnp.stack([ones, ones * cx, ones * ry]).reshape(3, pixels)
    terms = (cut[:, None] * poly[None]).reshape(3 * nimg, pixels)
    design = jnp.concatenate([terms, poly], axis=0)
    both = jnp.dot(
        design, jnp.concatenate([design, science], axis=0).T, precision=HI
    )
    gram = both[:, :-1]
    vector = both[:, -1]
    gram, vector = lax.psum((gram, vector), "tile")
    solution = solve_fit(gram, vector)

    weights = solution[: 3 * nimg].reshape(nimg, 3)
    cxf = col_coord[None, :]
    ryf = row_coord[:, None]
    flat = solution[3 * nimg] + solution[3 * nimg + 1] * cxf + solution[3 * nimg + 2] * ryf
    across = 0.0
    down = 0.0
    for k in range(nimg):
        flat = flat + weights[k, 0] * images[k]
        across = across + weights[k, 1] * images[k]
        down = down + weights[k, 2] * images[k]
    model = flat + cxf * across + ryf * down
    difference = image - model
    return (difference[None], solution[None])


def solution(mesh):
    return jax.shard_map(
        shards,
        mesh=mesh,
        in_specs=(
            P(("groups", "visit"), "tile", None),
            P("groups", None),
            P("groups", None),
            P(("groups", "visit"), "tile", None, None),
        ),
        out_specs=(P(("groups", "visit"), "tile", None), P(("groups", "visit"), None)),
        check_vma=False,
    )
```

```python
import numpy as np
import jax
import jax.numpy as jnp
from jax import lax
from jax.sharding import PartitionSpec as P
from jax.experimental import pallas as pl
from jax.experimental.pallas import tpu as pltpu

STAMP = 128
KERNEL = 31
HALF = KERNEL // 2
TERMS = 11
SHIFT = 32
LANE = 128
HI = lax.Precision.HIGHEST
CONV = lax.Precision.HIGH


RIDGE = 0.05
SIGMA_LIST = (1.0, 1.0, 1.0, 2.0, 2.0, 4.0)
POWER_LIST = (0, 1, 2, 0, 1, 0)
COLUMN_PICK = (0, 1, 0, 2, 1, 0, 3, 4, 3, 5)
ROW_PICK = (0, 0, 1, 0, 1, 2, 3, 3, 4, 5)


def profile_table():
    taps = np.arange(KERNEL, dtype=np.float64) - HALF
    stacked = []
    for sigma, power in zip(SIGMA_LIST, POWER_LIST):
        bell = np.exp(-taps * taps / (2.0 * sigma * sigma))
        stacked.append(bell * (taps / sigma) ** power / np.sum(bell))
    return np.stack(stacked)


def column_bands(table):
    spans = np.arange(2 * LANE)[:, None] - np.arange(LANE)[None, :]
    inside = (spans >= 0) & (spans < KERNEL)
    picked = table[:, np.clip(spans, 0, KERNEL - 1)]
    return np.where(inside[None], picked, 0.0).astype(np.float32)


def row_bands(table, height):
    spans = np.arange(height + 2 * HALF)[None, :] - np.arange(height)[:, None]
    inside = (spans >= 0) & (spans < KERNEL)
    picked = table[:, np.clip(spans, 0, KERNEL - 1)]
    return np.where(inside[None], picked, 0.0).astype(np.float32)


def coordinates(count, first, total):
    return (
        2.0 * (first + jnp.arange(count, dtype=jnp.int32)).astype(jnp.float32) + 1.0
    ) / total - 1.0


def solve_fit(gram, vector):
    regular = gram + RIDGE * jnp.diag(jnp.diag(gram))
    lower = jnp.linalg.cholesky(regular)
    return jax.scipy.linalg.cho_solve((lower, True), vector)


DIFF_ROWS = 32


def model_kernel(coef_ref, img_ref, exp_ref, row_ref, col_ref, out_ref):
    nimg = img_ref.shape[0]
    ry = row_ref[...]
    cx = col_ref[...]
    flat = coef_ref[3 * nimg] + coef_ref[3 * nimg + 1] * cx + coef_ref[3 * nimg + 2] * ry
    across = jnp.zeros(out_ref.shape, jnp.float32)
    down = jnp.zeros(out_ref.shape, jnp.float32)
    for k in range(nimg):
        plane = img_ref[k]
        flat = flat + coef_ref[3 * k] * plane
        across = across + coef_ref[3 * k + 1] * plane
        down = down + coef_ref[3 * k + 2] * plane
    out_ref[...] = exp_ref[...] - (flat + cx * across + ry * down)


def subtract_model(solution, images, image, row_coord, col_coord):
    nimg, height, width = images.shape
    return pl.pallas_call(
        model_kernel,
        grid=(height // DIFF_ROWS,),
        in_specs=[
            pl.BlockSpec(memory_space=pltpu.SMEM),
            pl.BlockSpec((nimg, DIFF_ROWS, width), lambda i: (0, i, 0)),
            pl.BlockSpec((DIFF_ROWS, width), lambda i: (i, 0)),
            pl.BlockSpec((DIFF_ROWS, 1), lambda i: (i, 0)),
            pl.BlockSpec((1, width), lambda i: (0, 0)),
        ],
        out_specs=pl.BlockSpec((DIFF_ROWS, width), lambda i: (i, 0)),
        out_shape=jax.ShapeDtypeStruct((height, width), jnp.float32),
    )(solution, images, image, row_coord[:, None], col_coord[None, :])


def shards(exposure, partners, offsets, stamps):
    visits = lax.axis_size("visit")
    tiles = lax.axis_size("tile")
    me = lax.axis_index("visit")
    my_tile = lax.axis_index("tile")
    image = exposure[0]
    height, width = image.shape
    block = height // visits
    chunks = -(-(width + 2 * HALF) // LANE)
    padded_width = chunks * LANE
    table = profile_table()

    blocks = image.reshape(visits, block, width)
    dest_rows = jnp.argmax(partners == me, axis=1).astype(jnp.int32)
    arrived = []
    for step in range(visits):
        target = (me + step) % visits
        piece = lax.dynamic_index_in_dim(blocks, dest_rows[target], 0, keepdims=True)
        if step:
            pairs = [(u, (u + step) % visits) for u in range(visits)]
            piece = lax.ppermute(piece, "visit", pairs)
        arrived.append(piece)
    recv = jnp.concatenate(arrived, axis=0)

    left = HALF + SHIFT
    right = 2 * SHIFT + padded_width - left - width
    recv_p = jnp.pad(recv, ((0, 0), (0, 0), (left, right)))
    my_steps = (me - partners[me]) % visits
    my_amounts = offsets[me]
    pieces = [
        lax.dynamic_slice(
            recv_p, (my_steps[r], 0, SHIFT + my_amounts[r]), (1, block, padded_width)
        )[0]
        for r in range(visits)
    ]
    columns = jnp.arange(padded_width, dtype=jnp.int32)
    keep = (columns >= HALF) & (columns < HALF + width)
    placed = jnp.where(keep[None, :], jnp.concatenate(pieces, axis=0), 0.0)

    forward = [(i, i + 1) for i in range(tiles - 1)]
    backward = [(i + 1, i) for i in range(tiles - 1)]
    above = lax.ppermute(placed[height - HALF :], "tile", forward)
    below = lax.ppermute(placed[:HALF], "tile", backward)
    field = jnp.concatenate([above, placed, below], axis=0)
    field_rows = height + 2 * HALF

    tiled = field.reshape(field_rows, chunks, LANE)
    windows = jnp.concatenate([tiled[:, : chunks - 1], tiled[:, 1:]], axis=-1)
    col_band = jnp.asarray(column_bands(table))
    filtered = [
        jnp.einsum("ybk,kx->ybx", windows, col_band[f], precision=CONV).reshape(
            field_rows, (chunks - 1) * LANE
        )[:, :width]
        for f in range(len(SIGMA_LIST))
    ]

    row_band = row_bands(table, height)
    found = {}
    for f in range(len(SIGMA_LIST)):
        terms = [k for k in range(len(COLUMN_PICK)) if COLUMN_PICK[k] == f]
        stacked_band = jnp.asarray(np.concatenate([row_band[ROW_PICK[k]] for k in terms]))
        out = jnp.dot(stacked_band, filtered[f], precision=CONV)
        for slot, k in enumerate(terms):
            found[k] = out[slot * height : (slot + 1) * height]
    images = jnp.stack([found[k] for k in range(len(COLUMN_PICK))])
    nimg = images.shape[0]

    row_coord = coordinates(height, my_tile * height, height * tiles)
    col_coord = coordinates(width, 0, width)

    anchors = stamps[0, 0]
    nstamp = anchors.shape[0]
    cuts, science, stamp_rows, stamp_cols = [], [], [], []
    for s in range(nstamp):
        row_start = anchors[s, 0]
        col_start = anchors[s, 1]
        cuts.append(lax.dynamic_slice(images, (0, row_start, col_start), (nimg, STAMP, STAMP)))
        science.append(lax.dynamic_slice(image, (row_start, col_start), (STAMP, STAMP)))
        stamp_rows.append(lax.dynamic_slice_in_dim(row_coord, row_start, STAMP))
        stamp_cols.append(lax.dynamic_slice_in_dim(col_coord, col_start, STAMP))
    cut = jnp.stack(cuts, axis=1).reshape(nimg, nstamp * STAMP, STAMP)
    science = jnp.stack(science).reshape(1, nstamp * STAMP, STAMP)
    ry = jnp.stack(stamp_rows)[:, :, None]
    cx = jnp.stack(stamp_cols)[:, None, :]
    ones = jnp.ones((nstamp, STAMP, STAMP), jnp.float32)
    poly = jnp.stack([ones, ones * cx, ones * ry]).reshape(3, nstamp * STAMP, STAMP)
    terms = (cut[:, None] * poly[None]).reshape(3 * nimg, nstamp * STAMP, STAMP)
    design = jnp.concatenate([terms, poly], axis=0)
    both = jnp.einsum(
        "ipx,jpx->ij", design, jnp.concatenate([design, science], axis=0), precision=HI
    )
    gram = both[:, :-1]
    vector = both[:, -1]
    gram, vector = lax.psum((gram, vector), "tile")
    solution = solve_fit(gram, vector)

    difference = subtract_model(solution, images, image, row_coord, col_coord)
    return (difference[None], solution[None])


def solution(mesh):
    return jax.shard_map(
        shards,
        mesh=mesh,
        in_specs=(
            P(("groups", "visit"), "tile", None),
            P("groups", None),
            P("groups", None),
            P(("groups", "visit"), "tile", None, None),
        ),
        out_specs=(P(("groups", "visit"), "tile", None), P(("groups", "visit"), None)),
        check_vma=False,
    )
```

```python
import numpy as np
import jax
import jax.numpy as jnp
from jax import lax
from jax.sharding import PartitionSpec as P
from jax.experimental import pallas as pl
from jax.experimental.pallas import tpu as pltpu

STAMP = 128
KERNEL = 31
HALF = KERNEL // 2
TERMS = 11
SHIFT = 32
LANE = 128
HI = lax.Precision.HIGHEST
CONV = lax.Precision.HIGH
GRAM = lax.Precision.HIGH


RIDGE = 0.05
SIGMA_LIST = (1.0, 1.0, 1.0, 2.0, 2.0, 4.0)
POWER_LIST = (0, 1, 2, 0, 1, 0)
COLUMN_PICK = (0, 1, 0, 2, 1, 0, 3, 4, 3, 5)
ROW_PICK = (0, 0, 1, 0, 1, 2, 3, 3, 4, 5)


def profile_table():
    taps = np.arange(KERNEL, dtype=np.float64) - HALF
    stacked = []
    for sigma, power in zip(SIGMA_LIST, POWER_LIST):
        bell = np.exp(-taps * taps / (2.0 * sigma * sigma))
        stacked.append(bell * (taps / sigma) ** power / np.sum(bell))
    return np.stack(stacked)


def column_bands(table):
    spans = np.arange(2 * LANE)[:, None] - np.arange(LANE)[None, :]
    inside = (spans >= 0) & (spans < KERNEL)
    picked = table[:, np.clip(spans, 0, KERNEL - 1)]
    return np.where(inside[None], picked, 0.0).astype(np.float32)


def row_bands(table, height):
    spans = np.arange(height + 2 * HALF)[None, :] - np.arange(height)[:, None]
    inside = (spans >= 0) & (spans < KERNEL)
    picked = table[:, np.clip(spans, 0, KERNEL - 1)]
    return np.where(inside[None], picked, 0.0).astype(np.float32)


def coordinates(count, first, total):
    return (
        2.0 * (first + jnp.arange(count, dtype=jnp.int32)).astype(jnp.float32) + 1.0
    ) / total - 1.0


def solve_fit(gram, vector):
    regular = gram + RIDGE * jnp.diag(jnp.diag(gram))
    lower = jnp.linalg.cholesky(regular)
    return jax.scipy.linalg.cho_solve((lower, True), vector)


DIFF_ROWS = 32


def model_kernel(coef_ref, img_ref, exp_ref, row_ref, col_ref, out_ref):
    nimg = img_ref.shape[0]
    ry = row_ref[...]
    cx = col_ref[...]
    flat = coef_ref[3 * nimg] + coef_ref[3 * nimg + 1] * cx + coef_ref[3 * nimg + 2] * ry
    across = jnp.zeros(out_ref.shape, jnp.float32)
    down = jnp.zeros(out_ref.shape, jnp.float32)
    for k in range(nimg):
        plane = img_ref[k]
        flat = flat + coef_ref[3 * k] * plane
        across = across + coef_ref[3 * k + 1] * plane
        down = down + coef_ref[3 * k + 2] * plane
    out_ref[...] = exp_ref[...] - (flat + cx * across + ry * down)


def subtract_model(solution, images, image, row_coord, col_coord):
    nimg, height, width = images.shape
    return pl.pallas_call(
        model_kernel,
        grid=(height // DIFF_ROWS,),
        in_specs=[
            pl.BlockSpec(memory_space=pltpu.SMEM),
            pl.BlockSpec((nimg, DIFF_ROWS, width), lambda i: (0, i, 0)),
            pl.BlockSpec((DIFF_ROWS, width), lambda i: (i, 0)),
            pl.BlockSpec((DIFF_ROWS, 1), lambda i: (i, 0)),
            pl.BlockSpec((1, width), lambda i: (0, 0)),
        ],
        out_specs=pl.BlockSpec((DIFF_ROWS, width), lambda i: (i, 0)),
        out_shape=jax.ShapeDtypeStruct((height, width), jnp.float32),
    )(solution, images, image, row_coord[:, None], col_coord[None, :])


def shards(exposure, partners, offsets, stamps):
    visits = lax.axis_size("visit")
    tiles = lax.axis_size("tile")
    me = lax.axis_index("visit")
    my_tile = lax.axis_index("tile")
    image = exposure[0]
    height, width = image.shape
    block = height // visits
    chunks = -(-(width + 2 * HALF) // LANE)
    padded_width = chunks * LANE
    table = profile_table()

    blocks = image.reshape(visits, block, width)
    dest_rows = jnp.argmax(partners == me, axis=1).astype(jnp.int32)
    arrived = []
    for step in range(visits):
        target = (me + step) % visits
        piece = lax.dynamic_index_in_dim(blocks, dest_rows[target], 0, keepdims=True)
        if step:
            pairs = [(u, (u + step) % visits) for u in range(visits)]
            piece = lax.ppermute(piece, "visit", pairs)
        arrived.append(piece)
    recv = jnp.concatenate(arrived, axis=0)

    left = HALF + SHIFT
    right = 2 * SHIFT + padded_width - left - width
    recv_p = jnp.pad(recv, ((0, 0), (0, 0), (left, right)))
    my_steps = (me - partners[me]) % visits
    my_amounts = offsets[me]
    pieces = [
        lax.dynamic_slice(
            recv_p, (my_steps[r], 0, SHIFT + my_amounts[r]), (1, block, padded_width)
        )[0]
        for r in range(visits)
    ]
    columns = jnp.arange(padded_width, dtype=jnp.int32)
    keep = (columns >= HALF) & (columns < HALF + width)
    placed = jnp.where(keep[None, :], jnp.concatenate(pieces, axis=0), 0.0)

    forward = [(i, i + 1) for i in range(tiles - 1)]
    backward = [(i + 1, i) for i in range(tiles - 1)]
    above = lax.ppermute(placed[height - HALF :], "tile", forward)
    below = lax.ppermute(placed[:HALF], "tile", backward)
    field = jnp.concatenate([above, placed, below], axis=0)
    field_rows = height + 2 * HALF

    tiled = field.reshape(field_rows, chunks, LANE)
    windows = jnp.concatenate([tiled[:, : chunks - 1], tiled[:, 1:]], axis=-1)
    col_band = jnp.asarray(column_bands(table))
    filtered = [
        jnp.einsum("ybk,kx->ybx", windows, col_band[f], precision=CONV).reshape(
            field_rows, (chunks - 1) * LANE
        )[:, :width]
        for f in range(len(SIGMA_LIST))
    ]

    row_band = row_bands(table, height)
    found = {}
    for f in range(len(SIGMA_LIST)):
        terms = [k for k in range(len(COLUMN_PICK)) if COLUMN_PICK[k] == f]
        stacked_band = jnp.asarray(np.concatenate([row_band[ROW_PICK[k]] for k in terms]))
        out = jnp.dot(stacked_band, filtered[f], precision=CONV)
        for slot, k in enumerate(terms):
            found[k] = out[slot * height : (slot + 1) * height]
    images = jnp.stack([found[k] for k in range(len(COLUMN_PICK))])
    nimg = images.shape[0]

    row_coord = coordinates(height, my_tile * height, height * tiles)
    col_coord = coordinates(width, 0, width)

    anchors = stamps[0, 0]
    nstamp = anchors.shape[0]
    cuts, science, stamp_rows, stamp_cols = [], [], [], []
    for s in range(nstamp):
        row_start = anchors[s, 0]
        col_start = anchors[s, 1]
        cuts.append(lax.dynamic_slice(images, (0, row_start, col_start), (nimg, STAMP, STAMP)))
        science.append(lax.dynamic_slice(image, (row_start, col_start), (STAMP, STAMP)))
        stamp_rows.append(lax.dynamic_slice_in_dim(row_coord, row_start, STAMP))
        stamp_cols.append(lax.dynamic_slice_in_dim(col_coord, col_start, STAMP))
    rows_all = nstamp * STAMP
    cut = jnp.stack([jnp.transpose(c, (1, 0, 2)) for c in cuts]).reshape(rows_all, nimg, STAMP)
    science = jnp.stack(science).reshape(rows_all, 1, STAMP)
    ry = jnp.stack(stamp_rows).reshape(rows_all, 1)
    cx = jnp.repeat(jnp.stack(stamp_cols), STAMP, axis=0)
    ones = jnp.ones((rows_all, STAMP), jnp.float32)
    poly = [ones, cx * ones, ry * ones]
    rows = [cut[:, k] * poly[a] for k in range(nimg) for a in range(3)] + poly
    design = jnp.stack(rows, axis=1)
    both = jnp.einsum(
        "pix,pjx->ij", design, jnp.concatenate([design, science], axis=1), precision=GRAM
    )
    gram = both[:, :-1]
    vector = both[:, -1]
    gram, vector = lax.psum((gram, vector), "tile")
    solution = solve_fit(gram, vector)

    difference = subtract_model(solution, images, image, row_coord, col_coord)
    return (difference[None], solution[None])


def solution(mesh):
    return jax.shard_map(
        shards,
        mesh=mesh,
        in_specs=(
            P(("groups", "visit"), "tile", None),
            P("groups", None),
            P("groups", None),
            P(("groups", "visit"), "tile", None, None),
        ),
        out_specs=(P(("groups", "visit"), "tile", None), P(("groups", "visit"), None)),
        check_vma=False,
    )
```

```python
import numpy as np
import jax
import jax.numpy as jnp
from jax import lax
from jax.sharding import PartitionSpec as P
from jax.experimental import pallas as pl
from jax.experimental.pallas import tpu as pltpu

STAMP = 128
KERNEL = 31
HALF = KERNEL // 2
TERMS = 11
SHIFT = 32
LANE = 128
HI = lax.Precision.HIGHEST
CONV = lax.Precision.HIGH


RIDGE = 0.05
SIGMA_LIST = (1.0, 1.0, 1.0, 2.0, 2.0, 4.0)
POWER_LIST = (0, 1, 2, 0, 1, 0)
COLUMN_PICK = (0, 1, 0, 2, 1, 0, 3, 4, 3, 5)
ROW_PICK = (0, 0, 1, 0, 1, 2, 3, 3, 4, 5)


def profile_table():
    taps = np.arange(KERNEL, dtype=np.float64) - HALF
    stacked = []
    for sigma, power in zip(SIGMA_LIST, POWER_LIST):
        bell = np.exp(-taps * taps / (2.0 * sigma * sigma))
        stacked.append(bell * (taps / sigma) ** power / np.sum(bell))
    return np.stack(stacked)


def column_bands(table):
    spans = np.arange(2 * LANE)[:, None] - np.arange(LANE)[None, :]
    inside = (spans >= 0) & (spans < KERNEL)
    picked = table[:, np.clip(spans, 0, KERNEL - 1)]
    return np.where(inside[None], picked, 0.0).astype(np.float32)


def row_bands(table, height):
    spans = np.arange(height + 2 * HALF)[None, :] - np.arange(height)[:, None]
    inside = (spans >= 0) & (spans < KERNEL)
    picked = table[:, np.clip(spans, 0, KERNEL - 1)]
    return np.where(inside[None], picked, 0.0).astype(np.float32)


def coordinates(count, first, total):
    return (
        2.0 * (first + jnp.arange(count, dtype=jnp.int32)).astype(jnp.float32) + 1.0
    ) / total - 1.0


def solve_fit(gram, vector):
    regular = gram + RIDGE * jnp.diag(jnp.diag(gram))
    lower = jnp.linalg.cholesky(regular)
    return jax.scipy.linalg.cho_solve((lower, True), vector)


DIFF_ROWS = 32


def model_kernel(coef_ref, img_ref, exp_ref, row_ref, col_ref, out_ref):
    nimg = img_ref.shape[0]
    ry = row_ref[...]
    cx = col_ref[...]
    flat = coef_ref[3 * nimg] + coef_ref[3 * nimg + 1] * cx + coef_ref[3 * nimg + 2] * ry
    across = jnp.zeros(out_ref.shape, jnp.float32)
    down = jnp.zeros(out_ref.shape, jnp.float32)
    for k in range(nimg):
        plane = img_ref[k]
        flat = flat + coef_ref[3 * k] * plane
        across = across + coef_ref[3 * k + 1] * plane
        down = down + coef_ref[3 * k + 2] * plane
    out_ref[...] = exp_ref[...] - (flat + cx * across + ry * down)


def subtract_model(solution, images, image, row_coord, col_coord):
    nimg, height, width = images.shape
    return pl.pallas_call(
        model_kernel,
        grid=(height // DIFF_ROWS,),
        in_specs=[
            pl.BlockSpec(memory_space=pltpu.SMEM),
            pl.BlockSpec((nimg, DIFF_ROWS, width), lambda i: (0, i, 0)),
            pl.BlockSpec((DIFF_ROWS, width), lambda i: (i, 0)),
            pl.BlockSpec((DIFF_ROWS, 1), lambda i: (i, 0)),
            pl.BlockSpec((1, width), lambda i: (0, 0)),
        ],
        out_specs=pl.BlockSpec((DIFF_ROWS, width), lambda i: (i, 0)),
        out_shape=jax.ShapeDtypeStruct((height, width), jnp.float32),
    )(solution, images, image, row_coord[:, None], col_coord[None, :])


def pick_kernel(rows_ref, blocks_ref, *out_refs):
    for step, out_ref in enumerate(out_refs):
        out_ref[...] = blocks_ref[rows_ref[step]]


def pick_blocks(rows, blocks):
    visits, block, width = blocks.shape
    return pl.pallas_call(
        pick_kernel,
        in_specs=[pl.BlockSpec(memory_space=pltpu.SMEM), pl.BlockSpec(memory_space=pltpu.VMEM)],
        out_shape=[jax.ShapeDtypeStruct((block, width), jnp.float32) for _ in range(visits)],
    )(rows, blocks)


def place_kernel(home_ref, amount_ref, *refs):
    arrived = refs[:-1]
    out_ref = refs[-1]
    block, padded_width = out_ref.shape[1:]
    columns = lax.broadcasted_iota(jnp.int32, (block, padded_width), 1)
    width = arrived[0].shape[1]
    keep = (columns >= HALF) & (columns < HALF + width)
    filler = jnp.zeros((block, padded_width - width), jnp.float32)
    for step, piece in enumerate(arrived):
        wide = jnp.concatenate([piece[...], filler], axis=1)
        turn = (HALF - amount_ref[step] + padded_width) % padded_width
        out_ref[home_ref[step]] = jnp.where(keep, pltpu.roll(wide, turn, 1), 0.0)


def place_blocks(home, amounts, arrived, padded_width):
    visits = len(arrived)
    block = arrived[0].shape[0]
    return pl.pallas_call(
        place_kernel,
        in_specs=[pl.BlockSpec(memory_space=pltpu.SMEM)] * 2
        + [pl.BlockSpec(memory_space=pltpu.VMEM)] * visits,
        out_shape=jax.ShapeDtypeStruct((visits, block, padded_width), jnp.float32),
    )(home, amounts, *arrived)


def shards(exposure, partners, offsets, stamps):
    visits = lax.axis_size("visit")
    tiles = lax.axis_size("tile")
    me = lax.axis_index("visit")
    my_tile = lax.axis_index("tile")
    image = exposure[0]
    height, width = image.shape
    block = height // visits
    chunks = -(-(width + 2 * HALF) // LANE)
    padded_width = chunks * LANE
    table = profile_table()

    blocks = image.reshape(visits, block, width)
    dest_rows = jnp.argmax(partners == me, axis=1).astype(jnp.int32)
    ahead = (me + jnp.arange(visits, dtype=jnp.int32)) % visits
    send_rows = dest_rows[ahead]
    my_sources = (me - jnp.arange(visits, dtype=jnp.int32)) % visits
    home = jnp.argmax(partners[me][None, :] == my_sources[:, None], axis=1).astype(jnp.int32)
    amounts = offsets[me][home].astype(jnp.int32)
    sent = pick_blocks(send_rows, blocks)
    arrived = [sent[0]]
    for step in range(1, visits):
        pairs = [(u, (u + step) % visits) for u in range(visits)]
        arrived.append(lax.ppermute(sent[step], "visit", pairs))
    placed = place_blocks(home, amounts, arrived, padded_width).reshape(height, padded_width)

    forward = [(i, i + 1) for i in range(tiles - 1)]
    backward = [(i + 1, i) for i in range(tiles - 1)]
    above = lax.ppermute(placed[height - HALF :], "tile", forward)
    below = lax.ppermute(placed[:HALF], "tile", backward)
    field = jnp.concatenate([above, placed, below], axis=0)
    field_rows = height + 2 * HALF

    tiled = field.reshape(field_rows, chunks, LANE)
    windows = jnp.concatenate([tiled[:, : chunks - 1], tiled[:, 1:]], axis=-1)
    col_band = jnp.asarray(column_bands(table))
    filtered = [
        jnp.einsum("ybk,kx->ybx", windows, col_band[f], precision=CONV).reshape(
            field_rows, (chunks - 1) * LANE
        )[:, :width]
        for f in range(len(SIGMA_LIST))
    ]

    row_band = row_bands(table, height)
    found = {}
    for f in range(len(SIGMA_LIST)):
        terms = [k for k in range(len(COLUMN_PICK)) if COLUMN_PICK[k] == f]
        stacked_band = jnp.asarray(np.concatenate([row_band[ROW_PICK[k]] for k in terms]))
        out = jnp.dot(stacked_band, filtered[f], precision=CONV)
        for slot, k in enumerate(terms):
            found[k] = out[slot * height : (slot + 1) * height]
    images = jnp.stack([found[k] for k in range(len(COLUMN_PICK))])
    nimg = images.shape[0]

    row_coord = coordinates(height, my_tile * height, height * tiles)
    col_coord = coordinates(width, 0, width)

    anchors = stamps[0, 0]
    nstamp = anchors.shape[0]
    cuts, science, stamp_rows, stamp_cols = [], [], [], []
    for s in range(nstamp):
        row_start = anchors[s, 0]
        col_start = anchors[s, 1]
        cuts.append(lax.dynamic_slice(images, (0, row_start, col_start), (nimg, STAMP, STAMP)))
        science.append(lax.dynamic_slice(image, (row_start, col_start), (STAMP, STAMP)))
        stamp_rows.append(lax.dynamic_slice_in_dim(row_coord, row_start, STAMP))
        stamp_cols.append(lax.dynamic_slice_in_dim(col_coord, col_start, STAMP))
    cut = jnp.stack(cuts, axis=1).reshape(nimg, nstamp * STAMP, STAMP)
    science = jnp.stack(science).reshape(1, nstamp * STAMP, STAMP)
    ry = jnp.stack(stamp_rows)[:, :, None]
    cx = jnp.stack(stamp_cols)[:, None, :]
    ones = jnp.ones((nstamp, STAMP, STAMP), jnp.float32)
    poly = jnp.stack([ones, ones * cx, ones * ry]).reshape(3, nstamp * STAMP, STAMP)
    terms = (cut[:, None] * poly[None]).reshape(3 * nimg, nstamp * STAMP, STAMP)
    design = jnp.concatenate([terms, poly], axis=0)
    both = jnp.einsum(
        "ipx,jpx->ij", design, jnp.concatenate([design, science], axis=0), precision=HI
    )
    gram = both[:, :-1]
    vector = both[:, -1]
    gram, vector = lax.psum((gram, vector), "tile")
    solution = solve_fit(gram, vector)

    difference = subtract_model(solution, images, image, row_coord, col_coord)
    return (difference[None], solution[None])


def solution(mesh):
    return jax.shard_map(
        shards,
        mesh=mesh,
        in_specs=(
            P(("groups", "visit"), "tile", None),
            P("groups", None),
            P("groups", None),
            P(("groups", "visit"), "tile", None, None),
        ),
        out_specs=(P(("groups", "visit"), "tile", None), P(("groups", "visit"), None)),
        check_vma=False,
    )
```

```python
import numpy as np
import jax
import jax.numpy as jnp
from jax import lax
from jax.sharding import PartitionSpec as P
from jax.experimental import pallas as pl
from jax.experimental.pallas import tpu as pltpu

STAMP = 128
KERNEL = 31
HALF = KERNEL // 2
TERMS = 11
SHIFT = 32
LANE = 128
HI = lax.Precision.HIGHEST
CONV = lax.Precision.HIGH


RIDGE = 0.05
SIGMA_LIST = (1.0, 1.0, 1.0, 2.0, 2.0, 4.0)
POWER_LIST = (0, 1, 2, 0, 1, 0)
COLUMN_PICK = (0, 1, 0, 2, 1, 0, 3, 4, 3, 5)
ROW_PICK = (0, 0, 1, 0, 1, 2, 3, 3, 4, 5)


def profile_table():
    taps = np.arange(KERNEL, dtype=np.float64) - HALF
    stacked = []
    for sigma, power in zip(SIGMA_LIST, POWER_LIST):
        bell = np.exp(-taps * taps / (2.0 * sigma * sigma))
        stacked.append(bell * (taps / sigma) ** power / np.sum(bell))
    return np.stack(stacked)


def column_bands(table):
    spans = np.arange(2 * LANE)[:, None] - np.arange(LANE)[None, :]
    inside = (spans >= 0) & (spans < KERNEL)
    picked = table[:, np.clip(spans, 0, KERNEL - 1)]
    return np.where(inside[None], picked, 0.0).astype(np.float32)


def row_bands(table, height):
    spans = np.arange(height + 2 * HALF)[None, :] - np.arange(height)[:, None]
    inside = (spans >= 0) & (spans < KERNEL)
    picked = table[:, np.clip(spans, 0, KERNEL - 1)]
    return np.where(inside[None], picked, 0.0).astype(np.float32)


def coordinates(count, first, total):
    return (
        2.0 * (first + jnp.arange(count, dtype=jnp.int32)).astype(jnp.float32) + 1.0
    ) / total - 1.0


def solve_fit(gram, vector):
    regular = gram + RIDGE * jnp.diag(jnp.diag(gram))
    lower = jnp.linalg.cholesky(regular)
    return jax.scipy.linalg.cho_solve((lower, True), vector)


DIFF_ROWS = 32


def model_kernel(coef_ref, img_ref, row_ref, col_ref, out_ref):
    nimg = img_ref.shape[0] - 1
    ry = row_ref[...]
    cx = col_ref[...]
    flat = coef_ref[3 * nimg] + coef_ref[3 * nimg + 1] * cx + coef_ref[3 * nimg + 2] * ry
    across = jnp.zeros(out_ref.shape, jnp.float32)
    down = jnp.zeros(out_ref.shape, jnp.float32)
    for k in range(nimg):
        plane = img_ref[k]
        flat = flat + coef_ref[3 * k] * plane
        across = across + coef_ref[3 * k + 1] * plane
        down = down + coef_ref[3 * k + 2] * plane
    out_ref[...] = img_ref[nimg] - (flat + cx * across + ry * down)


def subtract_model(solution, images, row_coord, col_coord):
    channels, height, width = images.shape
    return pl.pallas_call(
        model_kernel,
        grid=(height // DIFF_ROWS,),
        in_specs=[
            pl.BlockSpec(memory_space=pltpu.SMEM),
            pl.BlockSpec((channels, DIFF_ROWS, width), lambda i: (0, i, 0)),
            pl.BlockSpec((DIFF_ROWS, 1), lambda i: (i, 0)),
            pl.BlockSpec((1, width), lambda i: (0, 0)),
        ],
        out_specs=pl.BlockSpec((DIFF_ROWS, width), lambda i: (i, 0)),
        out_shape=jax.ShapeDtypeStruct((height, width), jnp.float32),
    )(solution, images, row_coord[:, None], col_coord[None, :])


def pick_kernel(rows_ref, blocks_ref, *out_refs):
    for step, out_ref in enumerate(out_refs):
        out_ref[...] = blocks_ref[rows_ref[step]]


def pick_blocks(rows, blocks):
    visits, block, width = blocks.shape
    return pl.pallas_call(
        pick_kernel,
        in_specs=[pl.BlockSpec(memory_space=pltpu.SMEM), pl.BlockSpec(memory_space=pltpu.VMEM)],
        out_shape=[jax.ShapeDtypeStruct((block, width), jnp.float32) for _ in range(visits)],
    )(rows, blocks)


def place_kernel(home_ref, amount_ref, *refs):
    arrived = refs[:-1]
    out_ref = refs[-1]
    block, padded_width = out_ref.shape[1:]
    columns = lax.broadcasted_iota(jnp.int32, (block, padded_width), 1)
    width = arrived[0].shape[1]
    keep = (columns >= HALF) & (columns < HALF + width)
    filler = jnp.zeros((block, padded_width - width), jnp.float32)
    for step, piece in enumerate(arrived):
        wide = jnp.concatenate([piece[...], filler], axis=1)
        turn = (HALF - amount_ref[step] + padded_width) % padded_width
        out_ref[home_ref[step]] = jnp.where(keep, pltpu.roll(wide, turn, 1), 0.0)


def place_blocks(home, amounts, arrived, padded_width):
    visits = len(arrived)
    block = arrived[0].shape[0]
    return pl.pallas_call(
        place_kernel,
        in_specs=[pl.BlockSpec(memory_space=pltpu.SMEM)] * 2
        + [pl.BlockSpec(memory_space=pltpu.VMEM)] * visits,
        out_shape=jax.ShapeDtypeStruct((visits, block, padded_width), jnp.float32),
    )(home, amounts, *arrived)


def shards(exposure, partners, offsets, stamps):
    visits = lax.axis_size("visit")
    tiles = lax.axis_size("tile")
    me = lax.axis_index("visit")
    my_tile = lax.axis_index("tile")
    image = exposure[0]
    height, width = image.shape
    block = height // visits
    chunks = -(-(width + 2 * HALF) // LANE)
    padded_width = chunks * LANE
    table = profile_table()

    blocks = image.reshape(visits, block, width)
    dest_rows = jnp.argmax(partners == me, axis=1).astype(jnp.int32)
    ahead = (me + jnp.arange(visits, dtype=jnp.int32)) % visits
    send_rows = dest_rows[ahead]
    my_sources = (me - jnp.arange(visits, dtype=jnp.int32)) % visits
    home = jnp.argmax(partners[me][None, :] == my_sources[:, None], axis=1).astype(jnp.int32)
    amounts = offsets[me][home].astype(jnp.int32)
    sent = pick_blocks(send_rows, blocks)
    arrived = [sent[0]]
    for step in range(1, visits):
        pairs = [(u, (u + step) % visits) for u in range(visits)]
        arrived.append(lax.ppermute(sent[step], "visit", pairs))
    placed = place_blocks(home, amounts, arrived, padded_width).reshape(height, padded_width)
    anchors, placed = lax.optimization_barrier((stamps[0, 0], placed))

    forward = [(i, i + 1) for i in range(tiles - 1)]
    backward = [(i + 1, i) for i in range(tiles - 1)]
    above = lax.ppermute(placed[height - HALF :], "tile", forward)
    below = lax.ppermute(placed[:HALF], "tile", backward)
    field = jnp.concatenate([above, placed, below], axis=0)
    field_rows = height + 2 * HALF

    tiled = field.reshape(field_rows, chunks, LANE)
    windows = jnp.concatenate([tiled[:, : chunks - 1], tiled[:, 1:]], axis=-1)
    col_band = jnp.asarray(column_bands(table))
    filtered = [
        jnp.einsum("ybk,kx->ybx", windows, col_band[f], precision=CONV).reshape(
            field_rows, (chunks - 1) * LANE
        )[:, :width]
        for f in range(len(SIGMA_LIST))
    ]

    row_band = row_bands(table, height)
    found = {}
    for f in range(len(SIGMA_LIST)):
        terms = [k for k in range(len(COLUMN_PICK)) if COLUMN_PICK[k] == f]
        stacked_band = jnp.asarray(np.concatenate([row_band[ROW_PICK[k]] for k in terms]))
        out = jnp.dot(stacked_band, filtered[f], precision=CONV)
        for slot, k in enumerate(terms):
            found[k] = out[slot * height : (slot + 1) * height]
    nimg = len(COLUMN_PICK)
    images = jnp.stack([found[k] for k in range(nimg)] + [image])

    row_coord = coordinates(height, my_tile * height, height * tiles)
    col_coord = coordinates(width, 0, width)

    nstamp = anchors.shape[0]
    cuts, stamp_rows, stamp_cols = [], [], []
    for s in range(nstamp):
        row_start = anchors[s, 0]
        col_start = anchors[s, 1]
        cuts.append(lax.dynamic_slice(images, (0, row_start, col_start), (nimg + 1, STAMP, STAMP)))
        stamp_rows.append(coordinates(STAMP, my_tile * height + row_start, height * tiles))
        stamp_cols.append(coordinates(STAMP, col_start, width))
    both_cut = jnp.stack(cuts, axis=1).reshape(nimg + 1, nstamp * STAMP, STAMP)
    cut = both_cut[:nimg]
    science = both_cut[nimg:]
    ry = jnp.stack(stamp_rows)[:, :, None]
    cx = jnp.stack(stamp_cols)[:, None, :]
    ones = jnp.ones((nstamp, STAMP, STAMP), jnp.float32)
    poly = jnp.stack([ones, ones * cx, ones * ry]).reshape(3, nstamp * STAMP, STAMP)
    terms = (cut[:, None] * poly[None]).reshape(3 * nimg, nstamp * STAMP, STAMP)
    design = jnp.concatenate([terms, poly], axis=0)
    both = jnp.einsum(
        "ipx,jpx->ij", design, jnp.concatenate([design, science], axis=0), precision=HI
    )
    gram = both[:, :-1]
    vector = both[:, -1]
    gram, vector = lax.psum((gram, vector), "tile")
    solution = solve_fit(gram, vector)

    difference = subtract_model(solution, images, row_coord, col_coord)
    return (difference[None], solution[None])


def solution(mesh):
    return jax.shard_map(
        shards,
        mesh=mesh,
        in_specs=(
            P(("groups", "visit"), "tile", None),
            P("groups", None),
            P("groups", None),
            P(("groups", "visit"), "tile", None, None),
        ),
        out_specs=(P(("groups", "visit"), "tile", None), P(("groups", "visit"), None)),
        check_vma=False,
    )
```

```python
import numpy as np
import jax
import jax.numpy as jnp
from jax import lax
from jax.sharding import PartitionSpec as P
from jax.experimental import pallas as pl
from jax.experimental.pallas import tpu as pltpu

STAMP = 128
KERNEL = 31
HALF = KERNEL // 2
TERMS = 11
SHIFT = 32
LANE = 128
HI = lax.Precision.HIGHEST
CONV = lax.Precision.HIGH


RIDGE = 0.05
SIGMA_LIST = (1.0, 1.0, 1.0, 2.0, 2.0, 4.0)
POWER_LIST = (0, 1, 2, 0, 1, 0)
COLUMN_PICK = (0, 1, 0, 2, 1, 0, 3, 4, 3, 5)
ROW_PICK = (0, 0, 1, 0, 1, 2, 3, 3, 4, 5)


def profile_table():
    taps = np.arange(KERNEL, dtype=np.float64) - HALF
    stacked = []
    for sigma, power in zip(SIGMA_LIST, POWER_LIST):
        bell = np.exp(-taps * taps / (2.0 * sigma * sigma))
        stacked.append(bell * (taps / sigma) ** power / np.sum(bell))
    return np.stack(stacked)


def column_bands(table):
    spans = np.arange(2 * LANE)[:, None] - np.arange(LANE)[None, :]
    inside = (spans >= 0) & (spans < KERNEL)
    picked = table[:, np.clip(spans, 0, KERNEL - 1)]
    return np.where(inside[None], picked, 0.0).astype(np.float32)


def row_bands(table, height):
    spans = np.arange(height + 2 * HALF)[None, :] - np.arange(height)[:, None]
    inside = (spans >= 0) & (spans < KERNEL)
    picked = table[:, np.clip(spans, 0, KERNEL - 1)]
    return np.where(inside[None], picked, 0.0).astype(np.float32)


def coordinates(count, first, total):
    return (
        2.0 * (first + jnp.arange(count, dtype=jnp.int32)).astype(jnp.float32) + 1.0
    ) / total - 1.0


def solve_fit(gram, vector):
    regular = gram + RIDGE * jnp.diag(jnp.diag(gram))
    lower = jnp.linalg.cholesky(regular)
    return jax.scipy.linalg.cho_solve((lower, True), vector)


DIFF_ROWS = 32


def model_kernel(coef_ref, img_ref, row_ref, col_ref, out_ref):
    nimg = img_ref.shape[0] - 1
    ry = row_ref[...]
    cx = col_ref[...]
    flat = coef_ref[3 * nimg] + coef_ref[3 * nimg + 1] * cx + coef_ref[3 * nimg + 2] * ry
    across = jnp.zeros(out_ref.shape, jnp.float32)
    down = jnp.zeros(out_ref.shape, jnp.float32)
    for k in range(nimg):
        plane = img_ref[k]
        flat = flat + coef_ref[3 * k] * plane
        across = across + coef_ref[3 * k + 1] * plane
        down = down + coef_ref[3 * k + 2] * plane
    out_ref[...] = img_ref[nimg] - (flat + cx * across + ry * down)


def subtract_model(solution, images, row_coord, col_coord):
    channels, height, width = images.shape
    return pl.pallas_call(
        model_kernel,
        grid=(height // DIFF_ROWS,),
        in_specs=[
            pl.BlockSpec(memory_space=pltpu.SMEM),
            pl.BlockSpec((channels, DIFF_ROWS, width), lambda i: (0, i, 0)),
            pl.BlockSpec((DIFF_ROWS, 1), lambda i: (i, 0)),
            pl.BlockSpec((1, width), lambda i: (0, 0)),
        ],
        out_specs=pl.BlockSpec((DIFF_ROWS, width), lambda i: (i, 0)),
        out_shape=jax.ShapeDtypeStruct((height, width), jnp.float32),
    )(solution, images, row_coord[:, None], col_coord[None, :])


def pick_kernel(rows_ref, blocks_ref, *out_refs):
    for step, out_ref in enumerate(out_refs):
        out_ref[...] = blocks_ref[rows_ref[step]]


def pick_blocks(rows, blocks):
    visits, block, width = blocks.shape
    return pl.pallas_call(
        pick_kernel,
        in_specs=[pl.BlockSpec(memory_space=pltpu.SMEM), pl.BlockSpec(memory_space=pltpu.VMEM)],
        out_shape=[jax.ShapeDtypeStruct((block, width), jnp.float32) for _ in range(visits)],
    )(rows, blocks)


def place_kernel(home_ref, amount_ref, *refs):
    arrived = refs[:-1]
    out_ref = refs[-1]
    block, padded_width = out_ref.shape[1:]
    columns = lax.broadcasted_iota(jnp.int32, (block, padded_width), 1)
    width = arrived[0].shape[1]
    keep = (columns >= HALF) & (columns < HALF + width)
    filler = jnp.zeros((block, padded_width - width), jnp.float32)
    for step, piece in enumerate(arrived):
        wide = jnp.concatenate([piece[...], filler], axis=1)
        turn = (HALF - amount_ref[step] + padded_width) % padded_width
        out_ref[home_ref[step]] = jnp.where(keep, pltpu.roll(wide, turn, 1), 0.0)


def place_blocks(home, amounts, arrived, padded_width):
    visits = len(arrived)
    block = arrived[0].shape[0]
    return pl.pallas_call(
        place_kernel,
        in_specs=[pl.BlockSpec(memory_space=pltpu.SMEM)] * 2
        + [pl.BlockSpec(memory_space=pltpu.VMEM)] * visits,
        out_shape=jax.ShapeDtypeStruct((visits, block, padded_width), jnp.float32),
    )(home, amounts, *arrived)


def shards(exposure, partners, offsets, stamps):
    visits = lax.axis_size("visit")
    tiles = lax.axis_size("tile")
    me = lax.axis_index("visit")
    my_tile = lax.axis_index("tile")
    image = exposure[0]
    height, width = image.shape
    block = height // visits
    chunks = -(-(width + 2 * HALF) // LANE)
    padded_width = chunks * LANE
    table = profile_table()

    blocks = image.reshape(visits, block, width)
    dest_rows = jnp.argmax(partners == me, axis=1).astype(jnp.int32)
    ahead = (me + jnp.arange(visits, dtype=jnp.int32)) % visits
    send_rows = dest_rows[ahead]
    my_sources = (me - jnp.arange(visits, dtype=jnp.int32)) % visits
    home = jnp.argmax(partners[me][None, :] == my_sources[:, None], axis=1).astype(jnp.int32)
    amounts = offsets[me][home].astype(jnp.int32)
    sent = pick_blocks(send_rows, blocks)
    arrived = [sent[0]]
    for step in range(1, visits):
        pairs = [(u, (u + step) % visits) for u in range(visits)]
        arrived.append(lax.ppermute(sent[step], "visit", pairs))
    placed = place_blocks(home, amounts, arrived, padded_width).reshape(height, padded_width)
    anchors, placed = lax.optimization_barrier((stamps[0, 0], placed))

    forward = [(i, i + 1) for i in range(tiles - 1)]
    backward = [(i + 1, i) for i in range(tiles - 1)]
    above = lax.ppermute(placed[height - HALF :], "tile", forward)
    below = lax.ppermute(placed[:HALF], "tile", backward)
    col_band = jnp.asarray(column_bands(table))
    nprof = len(SIGMA_LIST)

    def column_pass(rows):
        count = rows.shape[0]
        tiled = rows.reshape(count, chunks, LANE)
        windows = jnp.concatenate([tiled[:, : chunks - 1], tiled[:, 1:]], axis=-1)
        return [
            jnp.einsum("ybk,kx->ybx", windows, col_band[f], precision=CONV).reshape(
                count, (chunks - 1) * LANE
            )[:, :width]
            for f in range(nprof)
        ]

    filtered = column_pass(placed)
    row_band = row_bands(table, height)
    found = {}
    for f in range(nprof):
        terms = [k for k in range(len(COLUMN_PICK)) if COLUMN_PICK[k] == f]
        stacked_band = jnp.asarray(
            np.concatenate([row_band[ROW_PICK[k]][:, HALF : HALF + height] for k in terms])
        )
        out = jnp.dot(stacked_band, filtered[f], precision=CONV)
        for slot, k in enumerate(terms):
            found[k] = out[slot * height : (slot + 1) * height]

    edge = column_pass(jnp.concatenate([above, below], axis=0))
    fixes = []
    for k in range(len(COLUMN_PICK)):
        band_k = row_band[ROW_PICK[k]]
        top = jnp.asarray(band_k[:HALF, :HALF])
        bottom = jnp.asarray(band_k[height - HALF :, height + HALF :])
        src = edge[COLUMN_PICK[k]]
        fixes.append(
            (
                jnp.dot(top, src[:HALF], precision=CONV),
                jnp.dot(bottom, src[HALF:], precision=CONV),
            )
        )
    nimg = len(COLUMN_PICK)
    images = jnp.stack([found[k] for k in range(nimg)] + [image])
    top_fix = jnp.stack([f[0] for f in fixes])
    bottom_fix = jnp.stack([f[1] for f in fixes])
    images = images.at[:nimg, :HALF].add(top_fix).at[:nimg, height - HALF :].add(bottom_fix)

    row_coord = coordinates(height, my_tile * height, height * tiles)
    col_coord = coordinates(width, 0, width)

    nstamp = anchors.shape[0]
    cuts, stamp_rows, stamp_cols = [], [], []
    for s in range(nstamp):
        row_start = anchors[s, 0]
        col_start = anchors[s, 1]
        cuts.append(lax.dynamic_slice(images, (0, row_start, col_start), (nimg + 1, STAMP, STAMP)))
        stamp_rows.append(coordinates(STAMP, my_tile * height + row_start, height * tiles))
        stamp_cols.append(coordinates(STAMP, col_start, width))
    both_cut = jnp.stack(cuts, axis=1).reshape(nimg + 1, nstamp * STAMP, STAMP)
    cut = both_cut[:nimg]
    science = both_cut[nimg:]
    ry = jnp.stack(stamp_rows)[:, :, None]
    cx = jnp.stack(stamp_cols)[:, None, :]
    ones = jnp.ones((nstamp, STAMP, STAMP), jnp.float32)
    poly = jnp.stack([ones, ones * cx, ones * ry]).reshape(3, nstamp * STAMP, STAMP)
    terms = (cut[:, None] * poly[None]).reshape(3 * nimg, nstamp * STAMP, STAMP)
    design = jnp.concatenate([terms, poly], axis=0)
    both = jnp.einsum(
        "ipx,jpx->ij", design, jnp.concatenate([design, science], axis=0), precision=HI
    )
    gram = both[:, :-1]
    vector = both[:, -1]
    gram, vector = lax.psum((gram, vector), "tile")
    solution = solve_fit(gram, vector)

    difference = subtract_model(solution, images, row_coord, col_coord)
    return (difference[None], solution[None])


def solution(mesh):
    return jax.shard_map(
        shards,
        mesh=mesh,
        in_specs=(
            P(("groups", "visit"), "tile", None),
            P("groups", None),
            P("groups", None),
            P(("groups", "visit"), "tile", None, None),
        ),
        out_specs=(P(("groups", "visit"), "tile", None), P(("groups", "visit"), None)),
        check_vma=False,
    )
```

```python
import numpy as np
import jax
import jax.numpy as jnp
from jax import lax
from jax.sharding import PartitionSpec as P
from jax.experimental import pallas as pl
from jax.experimental.pallas import tpu as pltpu

STAMP = 128
KERNEL = 31
HALF = KERNEL // 2
TERMS = 11
SHIFT = 32
LANE = 128
HI = lax.Precision.HIGHEST
CONV = lax.Precision.HIGH


RIDGE = 0.05
SIGMA_LIST = (1.0, 1.0, 1.0, 2.0, 2.0, 4.0)
POWER_LIST = (0, 1, 2, 0, 1, 0)
COLUMN_PICK = (0, 1, 0, 2, 1, 0, 3, 4, 3, 5)
ROW_PICK = (0, 0, 1, 0, 1, 2, 3, 3, 4, 5)


def profile_table():
    taps = np.arange(KERNEL, dtype=np.float64) - HALF
    stacked = []
    for sigma, power in zip(SIGMA_LIST, POWER_LIST):
        bell = np.exp(-taps * taps / (2.0 * sigma * sigma))
        stacked.append(bell * (taps / sigma) ** power / np.sum(bell))
    return np.stack(stacked)


def column_bands(table):
    spans = np.arange(2 * LANE)[:, None] - np.arange(LANE)[None, :]
    inside = (spans >= 0) & (spans < KERNEL)
    picked = table[:, np.clip(spans, 0, KERNEL - 1)]
    return np.where(inside[None], picked, 0.0).astype(np.float32)


def row_bands(table, height):
    spans = np.arange(height + 2 * HALF)[None, :] - np.arange(height)[:, None]
    inside = (spans >= 0) & (spans < KERNEL)
    picked = table[:, np.clip(spans, 0, KERNEL - 1)]
    return np.where(inside[None], picked, 0.0).astype(np.float32)


def coordinates(count, first, total):
    return (
        2.0 * (first + jnp.arange(count, dtype=jnp.int32)).astype(jnp.float32) + 1.0
    ) / total - 1.0


def solve_fit(gram, vector):
    regular = gram + RIDGE * jnp.diag(jnp.diag(gram))
    lower = jnp.linalg.cholesky(regular)
    return jax.scipy.linalg.cho_solve((lower, True), vector)


DIFF_ROWS = 64


def model_kernel(coef_ref, img_ref, exp_ref, row_ref, col_ref, out_ref):
    nimg = img_ref.shape[0]
    ry = row_ref[...]
    cx = col_ref[...]
    flat = coef_ref[3 * nimg] + coef_ref[3 * nimg + 1] * cx + coef_ref[3 * nimg + 2] * ry
    across = jnp.zeros(out_ref.shape, jnp.float32)
    down = jnp.zeros(out_ref.shape, jnp.float32)
    for k in range(nimg):
        plane = img_ref[k]
        flat = flat + coef_ref[3 * k] * plane
        across = across + coef_ref[3 * k + 1] * plane
        down = down + coef_ref[3 * k + 2] * plane
    out_ref[...] = exp_ref[...] - (flat + cx * across + ry * down)


def subtract_model(solution, images, image, row_coord, col_coord):
    nimg, height, width = images.shape
    return pl.pallas_call(
        model_kernel,
        grid=(height // DIFF_ROWS,),
        in_specs=[
            pl.BlockSpec(memory_space=pltpu.SMEM),
            pl.BlockSpec((nimg, DIFF_ROWS, width), lambda i: (0, i, 0)),
            pl.BlockSpec((DIFF_ROWS, width), lambda i: (i, 0)),
            pl.BlockSpec((DIFF_ROWS, 1), lambda i: (i, 0)),
            pl.BlockSpec((1, width), lambda i: (0, 0)),
        ],
        out_specs=pl.BlockSpec((DIFF_ROWS, width), lambda i: (i, 0)),
        out_shape=jax.ShapeDtypeStruct((height, width), jnp.float32),
    )(solution, images, image, row_coord[:, None], col_coord[None, :])


def pick_kernel(rows_ref, blocks_ref, *out_refs):
    for step, out_ref in enumerate(out_refs):
        out_ref[...] = blocks_ref[rows_ref[step]]


def pick_blocks(rows, blocks):
    visits, block, width = blocks.shape
    return pl.pallas_call(
        pick_kernel,
        in_specs=[pl.BlockSpec(memory_space=pltpu.SMEM), pl.BlockSpec(memory_space=pltpu.VMEM)],
        out_shape=[jax.ShapeDtypeStruct((block, width), jnp.float32) for _ in range(visits)],
    )(rows, blocks)


def place_kernel(home_ref, amount_ref, *refs):
    arrived = refs[:-1]
    out_ref = refs[-1]
    block, padded_width = out_ref.shape[1:]
    columns = lax.broadcasted_iota(jnp.int32, (block, padded_width), 1)
    width = arrived[0].shape[1]
    keep = (columns >= HALF) & (columns < HALF + width)
    filler = jnp.zeros((block, padded_width - width), jnp.float32)
    for step, piece in enumerate(arrived):
        wide = jnp.concatenate([piece[...], filler], axis=1)
        turn = (HALF - amount_ref[step] + padded_width) % padded_width
        out_ref[home_ref[step]] = jnp.where(keep, pltpu.roll(wide, turn, 1), 0.0)


def place_blocks(home, amounts, arrived, padded_width):
    visits = len(arrived)
    block = arrived[0].shape[0]
    return pl.pallas_call(
        place_kernel,
        in_specs=[pl.BlockSpec(memory_space=pltpu.SMEM)] * 2
        + [pl.BlockSpec(memory_space=pltpu.VMEM)] * visits,
        out_shape=jax.ShapeDtypeStruct((visits, block, padded_width), jnp.float32),
    )(home, amounts, *arrived)


def shards(exposure, partners, offsets, stamps):
    visits = lax.axis_size("visit")
    tiles = lax.axis_size("tile")
    me = lax.axis_index("visit")
    my_tile = lax.axis_index("tile")
    image = exposure[0]
    height, width = image.shape
    block = height // visits
    chunks = -(-(width + 2 * HALF) // LANE)
    padded_width = chunks * LANE
    table = profile_table()

    blocks = image.reshape(visits, block, width)
    dest_rows = jnp.argmax(partners == me, axis=1).astype(jnp.int32)
    ahead = (me + jnp.arange(visits, dtype=jnp.int32)) % visits
    send_rows = dest_rows[ahead]
    my_sources = (me - jnp.arange(visits, dtype=jnp.int32)) % visits
    home = jnp.argmax(partners[me][None, :] == my_sources[:, None], axis=1).astype(jnp.int32)
    amounts = offsets[me][home].astype(jnp.int32)
    sent = pick_blocks(send_rows, blocks)
    arrived = [sent[0]]
    for step in range(1, visits):
        pairs = [(u, (u + step) % visits) for u in range(visits)]
        arrived.append(lax.ppermute(sent[step], "visit", pairs))
    placed = place_blocks(home, amounts, arrived, padded_width).reshape(height, padded_width)

    forward = [(i, i + 1) for i in range(tiles - 1)]
    backward = [(i + 1, i) for i in range(tiles - 1)]
    above = lax.ppermute(placed[height - HALF :], "tile", forward)
    below = lax.ppermute(placed[:HALF], "tile", backward)
    field = jnp.concatenate([above, placed, below], axis=0)
    field_rows = height + 2 * HALF

    tiled = field.reshape(field_rows, chunks, LANE)
    windows = jnp.concatenate([tiled[:, : chunks - 1], tiled[:, 1:]], axis=-1)
    col_band = jnp.asarray(column_bands(table))
    filtered = [
        jnp.einsum("ybk,kx->ybx", windows, col_band[f], precision=CONV).reshape(
            field_rows, (chunks - 1) * LANE
        )[:, :width]
        for f in range(len(SIGMA_LIST))
    ]

    row_band = row_bands(table, height)
    found = {}
    for f in range(len(SIGMA_LIST)):
        terms = [k for k in range(len(COLUMN_PICK)) if COLUMN_PICK[k] == f]
        stacked_band = jnp.asarray(np.concatenate([row_band[ROW_PICK[k]] for k in terms]))
        out = jnp.dot(stacked_band, filtered[f], precision=CONV)
        for slot, k in enumerate(terms):
            found[k] = out[slot * height : (slot + 1) * height]
    images = jnp.stack([found[k] for k in range(len(COLUMN_PICK))])
    nimg = images.shape[0]

    row_coord = coordinates(height, my_tile * height, height * tiles)
    col_coord = coordinates(width, 0, width)

    anchors = stamps[0, 0]
    nstamp = anchors.shape[0]
    cuts, science, stamp_rows, stamp_cols = [], [], [], []
    for s in range(nstamp):
        row_start = anchors[s, 0]
        col_start = anchors[s, 1]
        cuts.append(lax.dynamic_slice(images, (0, row_start, col_start), (nimg, STAMP, STAMP)))
        science.append(lax.dynamic_slice(image, (row_start, col_start), (STAMP, STAMP)))
        stamp_rows.append(lax.dynamic_slice_in_dim(row_coord, row_start, STAMP))
        stamp_cols.append(lax.dynamic_slice_in_dim(col_coord, col_start, STAMP))
    cut = jnp.stack(cuts, axis=1).reshape(nimg, nstamp * STAMP, STAMP)
    science = jnp.stack(science).reshape(1, nstamp * STAMP, STAMP)
    ry = jnp.stack(stamp_rows)[:, :, None]
    cx = jnp.stack(stamp_cols)[:, None, :]
    ones = jnp.ones((nstamp, STAMP, STAMP), jnp.float32)
    poly = jnp.stack([ones, ones * cx, ones * ry]).reshape(3, nstamp * STAMP, STAMP)
    terms = (cut[:, None] * poly[None]).reshape(3 * nimg, nstamp * STAMP, STAMP)
    design = jnp.concatenate([terms, poly], axis=0)
    both = jnp.einsum(
        "ipx,jpx->ij", design, jnp.concatenate([design, science], axis=0), precision=HI
    )
    gram = both[:, :-1]
    vector = both[:, -1]
    if tiles == 2:
        other = lax.ppermute(both, "tile", [(0, 1), (1, 0)])
        both = both + other
        gram = both[:, :-1]
        vector = both[:, -1]
    else:
        gram, vector = lax.psum((gram, vector), "tile")
    solution = solve_fit(gram, vector)

    difference = subtract_model(solution, images, image, row_coord, col_coord)
    return (difference[None], solution[None])


def solution(mesh):
    return jax.shard_map(
        shards,
        mesh=mesh,
        in_specs=(
            P(("groups", "visit"), "tile", None),
            P("groups", None),
            P("groups", None),
            P(("groups", "visit"), "tile", None, None),
        ),
        out_specs=(P(("groups", "visit"), "tile", None), P(("groups", "visit"), None)),
        check_vma=False,
    )
```

```python
import numpy as np
import jax
import jax.numpy as jnp
from jax import lax
from jax.sharding import PartitionSpec as P
from jax.experimental import pallas as pl
from jax.experimental.pallas import tpu as pltpu

STAMP = 128
KERNEL = 31
HALF = KERNEL // 2
TERMS = 11
SHIFT = 32
LANE = 128
HI = lax.Precision.HIGHEST
CONV = lax.Precision.HIGH


RIDGE = 0.05
SIGMA_LIST = (1.0, 1.0, 1.0, 2.0, 2.0, 4.0)
POWER_LIST = (0, 1, 2, 0, 1, 0)
COLUMN_PICK = (0, 1, 0, 2, 1, 0, 3, 4, 3, 5)
ROW_PICK = (0, 0, 1, 0, 1, 2, 3, 3, 4, 5)


def profile_table():
    taps = np.arange(KERNEL, dtype=np.float64) - HALF
    stacked = []
    for sigma, power in zip(SIGMA_LIST, POWER_LIST):
        bell = np.exp(-taps * taps / (2.0 * sigma * sigma))
        stacked.append(bell * (taps / sigma) ** power / np.sum(bell))
    return np.stack(stacked)


def column_bands(table):
    spans = np.arange(2 * LANE)[:, None] - np.arange(LANE)[None, :]
    inside = (spans >= 0) & (spans < KERNEL)
    picked = table[:, np.clip(spans, 0, KERNEL - 1)]
    return np.where(inside[None], picked, 0.0).astype(np.float32)


def row_bands(table, height):
    spans = np.arange(height + 2 * HALF)[None, :] - np.arange(height)[:, None]
    inside = (spans >= 0) & (spans < KERNEL)
    picked = table[:, np.clip(spans, 0, KERNEL - 1)]
    return np.where(inside[None], picked, 0.0).astype(np.float32)


def coordinates(count, first, total):
    return (
        2.0 * (first + jnp.arange(count, dtype=jnp.int32)).astype(jnp.float32) + 1.0
    ) / total - 1.0


def solve_fit(gram, vector):
    regular = gram + RIDGE * jnp.diag(jnp.diag(gram))
    lower = jnp.linalg.cholesky(regular)
    return jax.scipy.linalg.cho_solve((lower, True), vector)


DIFF_ROWS = 64


def model_kernel(coef_ref, img_ref, exp_ref, row_ref, col_ref, out_ref):
    nimg = img_ref.shape[0]
    ry = row_ref[...]
    cx = col_ref[...]
    flat = coef_ref[3 * nimg] + coef_ref[3 * nimg + 1] * cx + coef_ref[3 * nimg + 2] * ry
    across = jnp.zeros(out_ref.shape, jnp.float32)
    down = jnp.zeros(out_ref.shape, jnp.float32)
    for k in range(nimg):
        plane = img_ref[k]
        flat = flat + coef_ref[3 * k] * plane
        across = across + coef_ref[3 * k + 1] * plane
        down = down + coef_ref[3 * k + 2] * plane
    out_ref[...] = exp_ref[...] - (flat + cx * across + ry * down)


def subtract_model(solution, images, image, row_coord, col_coord):
    nimg, height, width = images.shape
    return pl.pallas_call(
        model_kernel,
        grid=(height // DIFF_ROWS,),
        in_specs=[
            pl.BlockSpec(memory_space=pltpu.SMEM),
            pl.BlockSpec((nimg, DIFF_ROWS, width), lambda i: (0, i, 0)),
            pl.BlockSpec((DIFF_ROWS, width), lambda i: (i, 0)),
            pl.BlockSpec((DIFF_ROWS, 1), lambda i: (i, 0)),
            pl.BlockSpec((1, width), lambda i: (0, 0)),
        ],
        out_specs=pl.BlockSpec((DIFF_ROWS, width), lambda i: (i, 0)),
        out_shape=jax.ShapeDtypeStruct((height, width), jnp.float32),
    )(solution, images, image, row_coord[:, None], col_coord[None, :])


def pick_kernel(rows_ref, blocks_ref, *out_refs):
    for step, out_ref in enumerate(out_refs):
        out_ref[...] = blocks_ref[rows_ref[step]]


def pick_blocks(rows, blocks):
    visits, block, width = blocks.shape
    return pl.pallas_call(
        pick_kernel,
        in_specs=[pl.BlockSpec(memory_space=pltpu.SMEM), pl.BlockSpec(memory_space=pltpu.VMEM)],
        out_shape=[jax.ShapeDtypeStruct((block, width), jnp.float32) for _ in range(visits)],
    )(rows, blocks)


def place_kernel(home_ref, amount_ref, *refs):
    arrived = refs[:-1]
    out_ref = refs[-1]
    block, padded_width = out_ref.shape[1:]
    columns = lax.broadcasted_iota(jnp.int32, (block, padded_width), 1)
    width = arrived[0].shape[1]
    keep = (columns >= HALF) & (columns < HALF + width)
    filler = jnp.zeros((block, padded_width - width), jnp.float32)
    for step, piece in enumerate(arrived):
        wide = jnp.concatenate([piece[...], filler], axis=1)
        turn = (HALF - amount_ref[step] + padded_width) % padded_width
        out_ref[home_ref[step]] = jnp.where(keep, pltpu.roll(wide, turn, 1), 0.0)


def place_blocks(home, amounts, arrived, padded_width):
    visits = len(arrived)
    block = arrived[0].shape[0]
    return pl.pallas_call(
        place_kernel,
        in_specs=[pl.BlockSpec(memory_space=pltpu.SMEM)] * 2
        + [pl.BlockSpec(memory_space=pltpu.VMEM)] * visits,
        out_shape=jax.ShapeDtypeStruct((visits, block, padded_width), jnp.float32),
    )(home, amounts, *arrived)


def shards(exposure, partners, offsets, stamps):
    visits = lax.axis_size("visit")
    tiles = lax.axis_size("tile")
    me = lax.axis_index("visit")
    my_tile = lax.axis_index("tile")
    image = exposure[0]
    height, width = image.shape
    block = height // visits
    chunks = -(-(width + 2 * HALF) // LANE)
    padded_width = chunks * LANE
    table = profile_table()

    blocks = image.reshape(visits, block, width)
    dest_rows = jnp.argmax(partners == me, axis=1).astype(jnp.int32)
    ahead = (me + jnp.arange(visits, dtype=jnp.int32)) % visits
    send_rows = dest_rows[ahead]
    my_sources = (me - jnp.arange(visits, dtype=jnp.int32)) % visits
    home = jnp.argmax(partners[me][None, :] == my_sources[:, None], axis=1).astype(jnp.int32)
    amounts = offsets[me][home].astype(jnp.int32)
    sent = pick_blocks(send_rows, blocks)
    arrived = [sent[0]]
    for step in range(1, visits):
        pairs = [(u, (u + step) % visits) for u in range(visits)]
        arrived.append(lax.ppermute(sent[step], "visit", pairs))
    placed = place_blocks(home, amounts, arrived, padded_width).reshape(height, padded_width)

    forward = [(i, i + 1) for i in range(tiles - 1)]
    backward = [(i + 1, i) for i in range(tiles - 1)]
    above = lax.ppermute(placed[height - HALF :], "tile", forward)
    below = lax.ppermute(placed[:HALF], "tile", backward)
    field = jnp.concatenate([above, placed, below], axis=0)
    field_rows = height + 2 * HALF

    tiled = field.reshape(field_rows, chunks, LANE)
    windows = jnp.concatenate([tiled[:, : chunks - 1], tiled[:, 1:]], axis=-1)
    col_band = jnp.asarray(column_bands(table))
    filtered = [
        jnp.einsum("ybk,kx->ybx", windows, col_band[f], precision=CONV).reshape(
            field_rows, (chunks - 1) * LANE
        )[:, :width]
        for f in range(len(SIGMA_LIST))
    ]

    row_band = row_bands(table, height)
    found = {}
    for f in range(len(SIGMA_LIST)):
        terms = [k for k in range(len(COLUMN_PICK)) if COLUMN_PICK[k] == f]
        stacked_band = jnp.asarray(np.concatenate([row_band[ROW_PICK[k]] for k in terms]))
        out = jnp.dot(stacked_band, filtered[f], precision=CONV)
        for slot, k in enumerate(terms):
            found[k] = out[slot * height : (slot + 1) * height]
    images = jnp.stack([found[k] for k in range(len(COLUMN_PICK))])
    nimg = images.shape[0]

    row_coord = coordinates(height, my_tile * height, height * tiles)
    col_coord = coordinates(width, 0, width)

    anchors = stamps[0, 0]
    nstamp = anchors.shape[0]
    cuts, science, stamp_rows, stamp_cols = [], [], [], []
    for s in range(nstamp):
        row_start = anchors[s, 0]
        col_start = anchors[s, 1]
        cuts.append(lax.dynamic_slice(images, (0, row_start, col_start), (nimg, STAMP, STAMP)))
        science.append(lax.dynamic_slice(image, (row_start, col_start), (STAMP, STAMP)))
        stamp_rows.append(lax.dynamic_slice_in_dim(row_coord, row_start, STAMP))
        stamp_cols.append(lax.dynamic_slice_in_dim(col_coord, col_start, STAMP))
    rows_all = nstamp * STAMP
    cut = jnp.stack(cuts, axis=1).reshape(nimg, rows_all, STAMP)
    group = 16
    channels = jnp.concatenate(
        [
            jnp.transpose(cut, (1, 0, 2)),
            jnp.stack(science).reshape(rows_all, 1, STAMP),
            jnp.ones((rows_all, 1, STAMP), jnp.float32),
            jnp.zeros((rows_all, group - nimg - 2, STAMP), jnp.float32),
        ],
        axis=1,
    )
    ry = jnp.stack(stamp_rows).reshape(rows_all, 1, 1)
    cx = jnp.repeat(jnp.stack(stamp_cols), STAMP, axis=0)[:, None, :]
    design = jnp.concatenate([channels, channels * cx, channels * ry], axis=1)
    big = jnp.einsum("pix,pjx->ij", design, design, precision=HI)
    order = np.array(
        [group * p + k for k in range(nimg) for p in range(3)]
        + [group * p + nimg + 1 for p in range(3)]
    )
    both = big[order[:, None], np.append(order, nimg)[None, :]]
    gram = both[:, :-1]
    vector = both[:, -1]
    if tiles == 2:
        other = lax.ppermute(both, "tile", [(0, 1), (1, 0)])
        both = both + other
        gram = both[:, :-1]
        vector = both[:, -1]
    else:
        gram, vector = lax.psum((gram, vector), "tile")
    solution = solve_fit(gram, vector)

    difference = subtract_model(solution, images, image, row_coord, col_coord)
    return (difference[None], solution[None])


def solution(mesh):
    return jax.shard_map(
        shards,
        mesh=mesh,
        in_specs=(
            P(("groups", "visit"), "tile", None),
            P("groups", None),
            P("groups", None),
            P(("groups", "visit"), "tile", None, None),
        ),
        out_specs=(P(("groups", "visit"), "tile", None), P(("groups", "visit"), None)),
        check_vma=False,
    )
```

```python
import numpy as np
import jax
import jax.numpy as jnp
from jax import lax
from jax.sharding import PartitionSpec as P
from jax.experimental import pallas as pl
from jax.experimental.pallas import tpu as pltpu

STAMP = 128
KERNEL = 31
HALF = KERNEL // 2
TERMS = 11
SHIFT = 32
LANE = 128
HI = lax.Precision.HIGHEST
CONV = lax.Precision.HIGH


RIDGE = 0.05
SIGMA_LIST = (1.0, 1.0, 1.0, 2.0, 2.0, 4.0)
POWER_LIST = (0, 1, 2, 0, 1, 0)
COLUMN_PICK = (0, 1, 0, 2, 1, 0, 3, 4, 3, 5)
ROW_PICK = (0, 0, 1, 0, 1, 2, 3, 3, 4, 5)


def profile_table():
    taps = np.arange(KERNEL, dtype=np.float64) - HALF
    stacked = []
    for sigma, power in zip(SIGMA_LIST, POWER_LIST):
        bell = np.exp(-taps * taps / (2.0 * sigma * sigma))
        stacked.append(bell * (taps / sigma) ** power / np.sum(bell))
    return np.stack(stacked)


def column_bands(table):
    spans = np.arange(2 * LANE)[:, None] - np.arange(LANE)[None, :]
    inside = (spans >= 0) & (spans < KERNEL)
    picked = table[:, np.clip(spans, 0, KERNEL - 1)]
    return np.where(inside[None], picked, 0.0).astype(np.float32)


def row_bands(table, height):
    spans = np.arange(height + 2 * HALF)[None, :] - np.arange(height)[:, None]
    inside = (spans >= 0) & (spans < KERNEL)
    picked = table[:, np.clip(spans, 0, KERNEL - 1)]
    return np.where(inside[None], picked, 0.0).astype(np.float32)


def coordinates(count, first, total):
    return (
        2.0 * (first + jnp.arange(count, dtype=jnp.int32)).astype(jnp.float32) + 1.0
    ) / total - 1.0


def solve_fit(gram, vector):
    regular = gram + RIDGE * jnp.diag(jnp.diag(gram))
    lower = jnp.linalg.cholesky(regular)
    return jax.scipy.linalg.cho_solve((lower, True), vector)


DIFF_ROWS = 64


def model_kernel(coef_ref, img_ref, exp_ref, row_ref, col_ref, out_ref):
    nimg = img_ref.shape[0]
    ry = row_ref[...]
    cx = col_ref[...]
    flat = coef_ref[3 * nimg] + coef_ref[3 * nimg + 1] * cx + coef_ref[3 * nimg + 2] * ry
    across = jnp.zeros(out_ref.shape, jnp.float32)
    down = jnp.zeros(out_ref.shape, jnp.float32)
    for k in range(nimg):
        plane = img_ref[k]
        flat = flat + coef_ref[3 * k] * plane
        across = across + coef_ref[3 * k + 1] * plane
        down = down + coef_ref[3 * k + 2] * plane
    out_ref[...] = exp_ref[...] - (flat + cx * across + ry * down)


def subtract_model(solution, images, image, row_coord, col_coord):
    nimg, height, width = images.shape
    return pl.pallas_call(
        model_kernel,
        grid=(height // DIFF_ROWS,),
        in_specs=[
            pl.BlockSpec(memory_space=pltpu.SMEM),
            pl.BlockSpec((nimg, DIFF_ROWS, width), lambda i: (0, i, 0)),
            pl.BlockSpec((DIFF_ROWS, width), lambda i: (i, 0)),
            pl.BlockSpec((DIFF_ROWS, 1), lambda i: (i, 0)),
            pl.BlockSpec((1, width), lambda i: (0, 0)),
        ],
        out_specs=pl.BlockSpec((DIFF_ROWS, width), lambda i: (i, 0)),
        out_shape=jax.ShapeDtypeStruct((height, width), jnp.float32),
    )(solution, images, image, row_coord[:, None], col_coord[None, :])


def pick_kernel(rows_ref, blocks_ref, *out_refs):
    for step, out_ref in enumerate(out_refs):
        out_ref[...] = blocks_ref[rows_ref[step]]


def pick_blocks(rows, blocks):
    visits, block, width = blocks.shape
    return pl.pallas_call(
        pick_kernel,
        in_specs=[pl.BlockSpec(memory_space=pltpu.SMEM), pl.BlockSpec(memory_space=pltpu.VMEM)],
        out_shape=[jax.ShapeDtypeStruct((block, width), jnp.float32) for _ in range(visits)],
    )(rows, blocks)


def place_kernel(home_ref, amount_ref, *refs):
    arrived = refs[:-1]
    out_ref = refs[-1]
    block, padded_width = out_ref.shape[1:]
    columns = lax.broadcasted_iota(jnp.int32, (block, padded_width), 1)
    width = arrived[0].shape[1]
    keep = (columns >= HALF) & (columns < HALF + width)
    filler = jnp.zeros((block, padded_width - width), jnp.float32)
    for step, piece in enumerate(arrived):
        wide = jnp.concatenate([piece[...], filler], axis=1)
        turn = (HALF - amount_ref[step] + padded_width) % padded_width
        out_ref[home_ref[step]] = jnp.where(keep, pltpu.roll(wide, turn, 1), 0.0)


def place_blocks(home, amounts, arrived, padded_width):
    visits = len(arrived)
    block = arrived[0].shape[0]
    return pl.pallas_call(
        place_kernel,
        in_specs=[pl.BlockSpec(memory_space=pltpu.SMEM)] * 2
        + [pl.BlockSpec(memory_space=pltpu.VMEM)] * visits,
        out_shape=jax.ShapeDtypeStruct((visits, block, padded_width), jnp.float32),
    )(home, amounts, *arrived)


def shards(exposure, partners, offsets, stamps):
    visits = lax.axis_size("visit")
    tiles = lax.axis_size("tile")
    me = lax.axis_index("visit")
    my_tile = lax.axis_index("tile")
    image = exposure[0]
    height, width = image.shape
    block = height // visits
    chunks = -(-(width + 2 * HALF) // LANE)
    padded_width = chunks * LANE
    table = profile_table()

    blocks = image.reshape(visits, block, width)
    dest_rows = jnp.argmax(partners == me, axis=1).astype(jnp.int32)
    ahead = (me + jnp.arange(visits, dtype=jnp.int32)) % visits
    send_rows = dest_rows[ahead]
    my_sources = (me - jnp.arange(visits, dtype=jnp.int32)) % visits
    home = jnp.argmax(partners[me][None, :] == my_sources[:, None], axis=1).astype(jnp.int32)
    amounts = offsets[me][home].astype(jnp.int32)
    sent = pick_blocks(send_rows, blocks)
    arrived = [sent[0]]
    for step in range(1, visits):
        pairs = [(u, (u + step) % visits) for u in range(visits)]
        arrived.append(lax.ppermute(sent[step], "visit", pairs))
    placed = place_blocks(home, amounts, arrived, padded_width).reshape(height, padded_width)

    forward = [(i, i + 1) for i in range(tiles - 1)]
    backward = [(i + 1, i) for i in range(tiles - 1)]
    above = lax.ppermute(placed[height - HALF :], "tile", forward)
    below = lax.ppermute(placed[:HALF], "tile", backward)
    field = jnp.concatenate([above, placed, below], axis=0)
    field_rows = height + 2 * HALF

    tiled = field.reshape(field_rows, chunks, LANE)
    windows = jnp.concatenate([tiled[:, : chunks - 1], tiled[:, 1:]], axis=-1)
    col_band = jnp.asarray(column_bands(table))
    filtered = [
        jnp.einsum("ybk,kx->ybx", windows, col_band[f], precision=CONV).reshape(
            field_rows, (chunks - 1) * LANE
        )[:, :width]
        for f in range(len(SIGMA_LIST))
    ]

    row_band = row_bands(table, height)
    found = {}
    for f in range(len(SIGMA_LIST)):
        terms = [k for k in range(len(COLUMN_PICK)) if COLUMN_PICK[k] == f]
        stacked_band = jnp.asarray(np.concatenate([row_band[ROW_PICK[k]] for k in terms]))
        out = jnp.dot(stacked_band, filtered[f], precision=CONV)
        for slot, k in enumerate(terms):
            found[k] = out[slot * height : (slot + 1) * height]
    images = jnp.stack([found[k] for k in range(len(COLUMN_PICK))])
    nimg = images.shape[0]

    row_coord = coordinates(height, my_tile * height, height * tiles)
    col_coord = coordinates(width, 0, width)

    anchors = stamps[0, 0]
    nstamp = anchors.shape[0]
    cuts, science, stamp_rows, stamp_cols = [], [], [], []
    for s in range(nstamp):
        row_start = anchors[s, 0]
        col_start = anchors[s, 1]
        cuts.append(lax.dynamic_slice(images, (0, row_start, col_start), (nimg, STAMP, STAMP)))
        science.append(lax.dynamic_slice(image, (row_start, col_start), (STAMP, STAMP)))
        stamp_rows.append(lax.dynamic_slice_in_dim(row_coord, row_start, STAMP))
        stamp_cols.append(lax.dynamic_slice_in_dim(col_coord, col_start, STAMP))
    pixels = nstamp * STAMP * STAMP
    cut = jnp.stack(cuts).reshape(nstamp, nimg, STAMP * STAMP)
    cut = jnp.transpose(cut, (1, 0, 2)).reshape(nimg, pixels)
    science = jnp.stack(science).reshape(1, pixels)
    flat = jnp.arange(pixels, dtype=jnp.int32)
    owner = flat // (STAMP * STAMP)
    pick = owner[None, :] == jnp.arange(nstamp, dtype=jnp.int32)[:, None]
    row_first = jnp.sum(jnp.where(pick, anchors[:, 0:1], 0), axis=0)
    col_first = jnp.sum(jnp.where(pick, anchors[:, 1:2], 0), axis=0)
    down = row_first + (flat // STAMP) % STAMP + my_tile * height
    across = col_first + flat % STAMP
    ry = (2.0 * down.astype(jnp.float32) + 1.0) / (height * tiles) - 1.0
    cx = (2.0 * across.astype(jnp.float32) + 1.0) / width - 1.0
    ones = jnp.ones((pixels,), jnp.float32)
    poly = [ones, cx, ry]
    design = jnp.stack([cut[k] * poly[p] for k in range(nimg) for p in range(3)] + poly)
    both = jnp.dot(design, jnp.concatenate([design, science], axis=0).T, precision=HI)
    gram = both[:, :-1]
    vector = both[:, -1]
    if tiles == 2:
        other = lax.ppermute(both, "tile", [(0, 1), (1, 0)])
        both = both + other
        gram = both[:, :-1]
        vector = both[:, -1]
    else:
        gram, vector = lax.psum((gram, vector), "tile")
    solution = solve_fit(gram, vector)

    difference = subtract_model(solution, images, image, row_coord, col_coord)
    return (difference[None], solution[None])


def solution(mesh):
    return jax.shard_map(
        shards,
        mesh=mesh,
        in_specs=(
            P(("groups", "visit"), "tile", None),
            P("groups", None),
            P("groups", None),
            P(("groups", "visit"), "tile", None, None),
        ),
        out_specs=(P(("groups", "visit"), "tile", None), P(("groups", "visit"), None)),
        check_vma=False,
    )
```

```python
import numpy as np
import jax
import jax.numpy as jnp
from jax import lax
from jax.sharding import PartitionSpec as P
from jax.experimental import pallas as pl
from jax.experimental.pallas import tpu as pltpu

STAMP = 128
KERNEL = 31
HALF = KERNEL // 2
TERMS = 11
SHIFT = 32
LANE = 128
HI = lax.Precision.HIGHEST
CONV = lax.Precision.HIGH


RIDGE = 0.05
SIGMA_LIST = (1.0, 1.0, 1.0, 2.0, 2.0, 4.0)
POWER_LIST = (0, 1, 2, 0, 1, 0)
COLUMN_PICK = (0, 1, 0, 2, 1, 0, 3, 4, 3, 5)
ROW_PICK = (0, 0, 1, 0, 1, 2, 3, 3, 4, 5)


def profile_table():
    taps = np.arange(KERNEL, dtype=np.float64) - HALF
    stacked = []
    for sigma, power in zip(SIGMA_LIST, POWER_LIST):
        bell = np.exp(-taps * taps / (2.0 * sigma * sigma))
        stacked.append(bell * (taps / sigma) ** power / np.sum(bell))
    return np.stack(stacked)


def column_bands(table):
    spans = np.arange(2 * LANE)[:, None] - np.arange(LANE)[None, :]
    inside = (spans >= 0) & (spans < KERNEL)
    picked = table[:, np.clip(spans, 0, KERNEL - 1)]
    return np.where(inside[None], picked, 0.0).astype(np.float32)


def row_bands(table, height):
    spans = np.arange(height + 2 * HALF)[None, :] - np.arange(height)[:, None]
    inside = (spans >= 0) & (spans < KERNEL)
    picked = table[:, np.clip(spans, 0, KERNEL - 1)]
    return np.where(inside[None], picked, 0.0).astype(np.float32)


def coordinates(count, first, total):
    return (
        2.0 * (first + jnp.arange(count, dtype=jnp.int32)).astype(jnp.float32) + 1.0
    ) / total - 1.0


def solve_fit(gram, vector):
    regular = gram + RIDGE * jnp.diag(jnp.diag(gram))
    lower = jnp.linalg.cholesky(regular)
    return jax.scipy.linalg.cho_solve((lower, True), vector)


DIFF_ROWS = 64


def model_kernel(coef_ref, img_ref, exp_ref, row_ref, col_ref, out_ref):
    nimg = img_ref.shape[0]
    ry = row_ref[...]
    cx = col_ref[...]
    flat = coef_ref[3 * nimg] + coef_ref[3 * nimg + 1] * cx + coef_ref[3 * nimg + 2] * ry
    across = jnp.zeros(out_ref.shape, jnp.float32)
    down = jnp.zeros(out_ref.shape, jnp.float32)
    for k in range(nimg):
        plane = img_ref[k]
        flat = flat + coef_ref[3 * k] * plane
        across = across + coef_ref[3 * k + 1] * plane
        down = down + coef_ref[3 * k + 2] * plane
    out_ref[...] = exp_ref[...] - (flat + cx * across + ry * down)


def subtract_model(solution, images, image, row_coord, col_coord):
    nimg, height, width = images.shape
    return pl.pallas_call(
        model_kernel,
        grid=(height // DIFF_ROWS,),
        in_specs=[
            pl.BlockSpec(memory_space=pltpu.SMEM),
            pl.BlockSpec((nimg, DIFF_ROWS, width), lambda i: (0, i, 0)),
            pl.BlockSpec((DIFF_ROWS, width), lambda i: (i, 0)),
            pl.BlockSpec((DIFF_ROWS, 1), lambda i: (i, 0)),
            pl.BlockSpec((1, width), lambda i: (0, 0)),
        ],
        out_specs=pl.BlockSpec((DIFF_ROWS, width), lambda i: (i, 0)),
        out_shape=jax.ShapeDtypeStruct((height, width), jnp.float32),
    )(solution, images, image, row_coord[:, None], col_coord[None, :])


def pick_kernel(rows_ref, blocks_ref, *out_refs):
    for step, out_ref in enumerate(out_refs):
        out_ref[...] = blocks_ref[rows_ref[step]]


def pick_blocks(rows, blocks):
    visits, block, width = blocks.shape
    return pl.pallas_call(
        pick_kernel,
        in_specs=[pl.BlockSpec(memory_space=pltpu.SMEM), pl.BlockSpec(memory_space=pltpu.VMEM)],
        out_shape=[jax.ShapeDtypeStruct((block, width), jnp.float32) for _ in range(visits)],
    )(rows, blocks)


def place_kernel(home_ref, amount_ref, *refs):
    arrived = refs[:-1]
    out_ref = refs[-1]
    block, padded_width = out_ref.shape[1:]
    columns = lax.broadcasted_iota(jnp.int32, (block, padded_width), 1)
    width = arrived[0].shape[1]
    keep = (columns >= HALF) & (columns < HALF + width)
    filler = jnp.zeros((block, padded_width - width), jnp.float32)
    for step, piece in enumerate(arrived):
        wide = jnp.concatenate([piece[...], filler], axis=1)
        turn = (HALF - amount_ref[step] + padded_width) % padded_width
        out_ref[home_ref[step]] = jnp.where(keep, pltpu.roll(wide, turn, 1), 0.0)


def place_blocks(home, amounts, arrived, padded_width):
    visits = len(arrived)
    block = arrived[0].shape[0]
    return pl.pallas_call(
        place_kernel,
        in_specs=[pl.BlockSpec(memory_space=pltpu.SMEM)] * 2
        + [pl.BlockSpec(memory_space=pltpu.VMEM)] * visits,
        out_shape=jax.ShapeDtypeStruct((visits, block, padded_width), jnp.float32),
    )(home, amounts, *arrived)


def shards(exposure, partners, offsets, stamps):
    visits = lax.axis_size("visit")
    tiles = lax.axis_size("tile")
    me = lax.axis_index("visit")
    my_tile = lax.axis_index("tile")
    image = exposure[0]
    height, width = image.shape
    block = height // visits
    chunks = -(-(width + 2 * HALF) // LANE)
    padded_width = chunks * LANE
    table = profile_table()

    blocks = image.reshape(visits, block, width)
    dest_rows = jnp.argmax(partners == me, axis=1).astype(jnp.int32)
    ahead = (me + jnp.arange(visits, dtype=jnp.int32)) % visits
    send_rows = dest_rows[ahead]
    my_sources = (me - jnp.arange(visits, dtype=jnp.int32)) % visits
    home = jnp.argmax(partners[me][None, :] == my_sources[:, None], axis=1).astype(jnp.int32)
    amounts = offsets[me][home].astype(jnp.int32)
    sent = pick_blocks(send_rows, blocks)
    arrived = [sent[0]]
    for step in range(1, visits):
        pairs = [(u, (u + step) % visits) for u in range(visits)]
        arrived.append(lax.ppermute(sent[step], "visit", pairs))
    placed = place_blocks(home, amounts, arrived, padded_width).reshape(height, padded_width)

    forward = [(i, i + 1) for i in range(tiles - 1)]
    backward = [(i + 1, i) for i in range(tiles - 1)]
    above = lax.ppermute(placed[height - HALF :], "tile", forward)
    below = lax.ppermute(placed[:HALF], "tile", backward)
    field = jnp.concatenate([above, placed, below], axis=0)
    field_rows = height + 2 * HALF

    tiled = field.reshape(field_rows, chunks, LANE)
    windows = jnp.concatenate([tiled[:, : chunks - 1], tiled[:, 1:]], axis=-1)
    col_band = jnp.asarray(column_bands(table))
    filtered = [
        jnp.einsum("ybk,kx->ybx", windows, col_band[f], precision=CONV).reshape(
            field_rows, (chunks - 1) * LANE
        )[:, :width]
        for f in range(len(SIGMA_LIST))
    ]

    chunk_rows = STAMP if height % STAMP == 0 else height
    row_band = row_bands(table, chunk_rows)
    found = {}
    for f in range(len(SIGMA_LIST)):
        terms = [k for k in range(len(COLUMN_PICK)) if COLUMN_PICK[k] == f]
        stacked_band = jnp.asarray(np.concatenate([row_band[ROW_PICK[k]] for k in terms]))
        outs = [
            jnp.dot(
                stacked_band,
                filtered[f][q : q + chunk_rows + 2 * HALF],
                precision=CONV,
            )
            for q in range(0, height, chunk_rows)
        ]
        for slot, k in enumerate(terms):
            found[k] = jnp.concatenate(
                [o[slot * chunk_rows : (slot + 1) * chunk_rows] for o in outs], axis=0
            )
    images = jnp.stack([found[k] for k in range(len(COLUMN_PICK))])
    nimg = images.shape[0]

    row_coord = coordinates(height, my_tile * height, height * tiles)
    col_coord = coordinates(width, 0, width)

    anchors = stamps[0, 0]
    nstamp = anchors.shape[0]
    cuts, science, stamp_rows, stamp_cols = [], [], [], []
    for s in range(nstamp):
        row_start = anchors[s, 0]
        col_start = anchors[s, 1]
        cuts.append(lax.dynamic_slice(images, (0, row_start, col_start), (nimg, STAMP, STAMP)))
        science.append(lax.dynamic_slice(image, (row_start, col_start), (STAMP, STAMP)))
        stamp_rows.append(lax.dynamic_slice_in_dim(row_coord, row_start, STAMP))
        stamp_cols.append(lax.dynamic_slice_in_dim(col_coord, col_start, STAMP))
    cut = jnp.stack(cuts, axis=1).reshape(nimg, nstamp * STAMP, STAMP)
    science = jnp.stack(science).reshape(1, nstamp * STAMP, STAMP)
    ry = jnp.stack(stamp_rows)[:, :, None]
    cx = jnp.stack(stamp_cols)[:, None, :]
    ones = jnp.ones((nstamp, STAMP, STAMP), jnp.float32)
    poly = jnp.stack([ones, ones * cx, ones * ry]).reshape(3, nstamp * STAMP, STAMP)
    terms = (cut[:, None] * poly[None]).reshape(3 * nimg, nstamp * STAMP, STAMP)
    design = jnp.concatenate([terms, poly], axis=0)
    both = jnp.einsum(
        "ipx,jpx->ij", design, jnp.concatenate([design, science], axis=0), precision=HI
    )
    gram = both[:, :-1]
    vector = both[:, -1]
    if tiles == 2:
        other = lax.ppermute(both, "tile", [(0, 1), (1, 0)])
        both = both + other
        gram = both[:, :-1]
        vector = both[:, -1]
    else:
        gram, vector = lax.psum((gram, vector), "tile")
    solution = solve_fit(gram, vector)

    difference = subtract_model(solution, images, image, row_coord, col_coord)
    return (difference[None], solution[None])


def solution(mesh):
    return jax.shard_map(
        shards,
        mesh=mesh,
        in_specs=(
            P(("groups", "visit"), "tile", None),
            P("groups", None),
            P("groups", None),
            P(("groups", "visit"), "tile", None, None),
        ),
        out_specs=(P(("groups", "visit"), "tile", None), P(("groups", "visit"), None)),
        check_vma=False,
    )
```

```python
import numpy as np
import jax
import jax.numpy as jnp
from jax import lax
from jax.sharding import PartitionSpec as P
from jax.experimental import pallas as pl
from jax.experimental.pallas import tpu as pltpu

STAMP = 128
KERNEL = 31
HALF = KERNEL // 2
TERMS = 11
SHIFT = 32
LANE = 128
HI = lax.Precision.HIGHEST
CONV = lax.Precision.HIGH


RIDGE = 0.05
SIGMA_LIST = (1.0, 1.0, 1.0, 2.0, 2.0, 4.0)
POWER_LIST = (0, 1, 2, 0, 1, 0)
COLUMN_PICK = (0, 1, 0, 2, 1, 0, 3, 4, 3, 5)
ROW_PICK = (0, 0, 1, 0, 1, 2, 3, 3, 4, 5)


def profile_table():
    taps = np.arange(KERNEL, dtype=np.float64) - HALF
    stacked = []
    for sigma, power in zip(SIGMA_LIST, POWER_LIST):
        bell = np.exp(-taps * taps / (2.0 * sigma * sigma))
        stacked.append(bell * (taps / sigma) ** power / np.sum(bell))
    return np.stack(stacked)


def column_bands(table):
    spans = np.arange(2 * LANE)[:, None] - np.arange(LANE)[None, :]
    inside = (spans >= 0) & (spans < KERNEL)
    picked = table[:, np.clip(spans, 0, KERNEL - 1)]
    return np.where(inside[None], picked, 0.0).astype(np.float32)


def row_bands(table, height):
    spans = np.arange(height + 2 * HALF)[None, :] - np.arange(height)[:, None]
    inside = (spans >= 0) & (spans < KERNEL)
    picked = table[:, np.clip(spans, 0, KERNEL - 1)]
    return np.where(inside[None], picked, 0.0).astype(np.float32)


def coordinates(count, first, total):
    return (
        2.0 * (first + jnp.arange(count, dtype=jnp.int32)).astype(jnp.float32) + 1.0
    ) / total - 1.0


def solve_fit(gram, vector):
    regular = gram + RIDGE * jnp.diag(jnp.diag(gram))
    lower = jnp.linalg.cholesky(regular)
    return jax.scipy.linalg.cho_solve((lower, True), vector)


DIFF_ROWS = 64


def model_kernel(coef_ref, img_ref, exp_ref, row_ref, col_ref, out_ref):
    nimg = img_ref.shape[0]
    ry = row_ref[...]
    cx = col_ref[...]
    flat = coef_ref[3 * nimg] + coef_ref[3 * nimg + 1] * cx + coef_ref[3 * nimg + 2] * ry
    across = jnp.zeros(out_ref.shape, jnp.float32)
    down = jnp.zeros(out_ref.shape, jnp.float32)
    for k in range(nimg):
        plane = img_ref[k]
        flat = flat + coef_ref[3 * k] * plane
        across = across + coef_ref[3 * k + 1] * plane
        down = down + coef_ref[3 * k + 2] * plane
    out_ref[...] = exp_ref[...] - (flat + cx * across + ry * down)


def subtract_model(solution, images, image, row_coord, col_coord):
    nimg, height, width = images.shape
    return pl.pallas_call(
        model_kernel,
        grid=(height // DIFF_ROWS,),
        in_specs=[
            pl.BlockSpec(memory_space=pltpu.SMEM),
            pl.BlockSpec((nimg, DIFF_ROWS, width), lambda i: (0, i, 0)),
            pl.BlockSpec((DIFF_ROWS, width), lambda i: (i, 0)),
            pl.BlockSpec((DIFF_ROWS, 1), lambda i: (i, 0)),
            pl.BlockSpec((1, width), lambda i: (0, 0)),
        ],
        out_specs=pl.BlockSpec((DIFF_ROWS, width), lambda i: (i, 0)),
        out_shape=jax.ShapeDtypeStruct((height, width), jnp.float32),
    )(solution, images, image, row_coord[:, None], col_coord[None, :])


def pick_kernel(rows_ref, blocks_ref, *out_refs):
    for step, out_ref in enumerate(out_refs):
        out_ref[...] = blocks_ref[rows_ref[step]]


def pick_blocks(rows, blocks):
    visits, block, width = blocks.shape
    return pl.pallas_call(
        pick_kernel,
        in_specs=[pl.BlockSpec(memory_space=pltpu.SMEM), pl.BlockSpec(memory_space=pltpu.VMEM)],
        out_shape=[jax.ShapeDtypeStruct((block, width), jnp.float32) for _ in range(visits)],
    )(rows, blocks)


def place_kernel(home_ref, amount_ref, *refs):
    arrived = refs[:-1]
    out_ref = refs[-1]
    block, padded_width = out_ref.shape[1:]
    columns = lax.broadcasted_iota(jnp.int32, (block, padded_width), 1)
    width = arrived[0].shape[1]
    keep = (columns >= HALF) & (columns < HALF + width)
    filler = jnp.zeros((block, padded_width - width), jnp.float32)
    for step, piece in enumerate(arrived):
        wide = jnp.concatenate([piece[...], filler], axis=1)
        turn = (HALF - amount_ref[step] + padded_width) % padded_width
        out_ref[home_ref[step]] = jnp.where(keep, pltpu.roll(wide, turn, 1), 0.0)


def place_blocks(home, amounts, arrived, padded_width):
    visits = len(arrived)
    block = arrived[0].shape[0]
    return pl.pallas_call(
        place_kernel,
        in_specs=[pl.BlockSpec(memory_space=pltpu.SMEM)] * 2
        + [pl.BlockSpec(memory_space=pltpu.VMEM)] * visits,
        out_shape=jax.ShapeDtypeStruct((visits, block, padded_width), jnp.float32),
    )(home, amounts, *arrived)


def shards(exposure, partners, offsets, stamps):
    visits = lax.axis_size("visit")
    tiles = lax.axis_size("tile")
    me = lax.axis_index("visit")
    my_tile = lax.axis_index("tile")
    image = exposure[0]
    height, width = image.shape
    block = height // visits
    chunks = -(-(width + 2 * HALF) // LANE)
    padded_width = chunks * LANE
    table = profile_table()

    blocks = image.reshape(visits, block, width)
    dest_rows = jnp.argmax(partners == me, axis=1).astype(jnp.int32)
    ahead = (me + jnp.arange(visits, dtype=jnp.int32)) % visits
    send_rows = dest_rows[ahead]
    my_sources = (me - jnp.arange(visits, dtype=jnp.int32)) % visits
    home = jnp.argmax(partners[me][None, :] == my_sources[:, None], axis=1).astype(jnp.int32)
    amounts = offsets[me][home].astype(jnp.int32)
    row_coord = coordinates(height, my_tile * height, height * tiles)
    col_coord = coordinates(width, 0, width)
    anchors = stamps[0, 0]
    nstamp = anchors.shape[0]
    science, stamp_rows, stamp_cols = [], [], []
    for s in range(nstamp):
        row_start = anchors[s, 0]
        col_start = anchors[s, 1]
        science.append(lax.dynamic_slice(image, (row_start, col_start), (STAMP, STAMP)))
        stamp_rows.append(lax.dynamic_slice_in_dim(row_coord, row_start, STAMP))
        stamp_cols.append(lax.dynamic_slice_in_dim(col_coord, col_start, STAMP))
    science, stamp_rows, stamp_cols, blocks = lax.optimization_barrier(
        (jnp.stack(science), jnp.stack(stamp_rows), jnp.stack(stamp_cols), blocks)
    )
    sent = pick_blocks(send_rows, blocks)
    arrived = [sent[0]]
    for step in range(1, visits):
        pairs = [(u, (u + step) % visits) for u in range(visits)]
        arrived.append(lax.ppermute(sent[step], "visit", pairs))
    placed = place_blocks(home, amounts, arrived, padded_width).reshape(height, padded_width)

    forward = [(i, i + 1) for i in range(tiles - 1)]
    backward = [(i + 1, i) for i in range(tiles - 1)]
    above = lax.ppermute(placed[height - HALF :], "tile", forward)
    below = lax.ppermute(placed[:HALF], "tile", backward)
    field = jnp.concatenate([above, placed, below], axis=0)
    field_rows = height + 2 * HALF

    tiled = field.reshape(field_rows, chunks, LANE)
    windows = jnp.concatenate([tiled[:, : chunks - 1], tiled[:, 1:]], axis=-1)
    col_band = jnp.asarray(column_bands(table))
    filtered = [
        jnp.einsum("ybk,kx->ybx", windows, col_band[f], precision=CONV).reshape(
            field_rows, (chunks - 1) * LANE
        )[:, :width]
        for f in range(len(SIGMA_LIST))
    ]

    chunk_rows = STAMP if height % STAMP == 0 else height
    row_band = row_bands(table, chunk_rows)
    found = {}
    for f in range(len(SIGMA_LIST)):
        terms = [k for k in range(len(COLUMN_PICK)) if COLUMN_PICK[k] == f]
        stacked_band = jnp.asarray(np.concatenate([row_band[ROW_PICK[k]] for k in terms]))
        outs = [
            jnp.dot(
                stacked_band,
                filtered[f][q : q + chunk_rows + 2 * HALF],
                precision=CONV,
            )
            for q in range(0, height, chunk_rows)
        ]
        for slot, k in enumerate(terms):
            found[k] = jnp.concatenate(
                [o[slot * chunk_rows : (slot + 1) * chunk_rows] for o in outs], axis=0
            )
    images = jnp.stack([found[k] for k in range(len(COLUMN_PICK))])
    nimg = images.shape[0]


    cuts = [
        lax.dynamic_slice(images, (0, anchors[s, 0], anchors[s, 1]), (nimg, STAMP, STAMP))
        for s in range(nstamp)
    ]
    cut = jnp.stack(cuts, axis=1).reshape(nimg, nstamp * STAMP, STAMP)
    science = science.reshape(1, nstamp * STAMP, STAMP)
    ry = stamp_rows[:, :, None]
    cx = stamp_cols[:, None, :]
    ones = jnp.ones((nstamp, STAMP, STAMP), jnp.float32)
    poly = jnp.stack([ones, ones * cx, ones * ry]).reshape(3, nstamp * STAMP, STAMP)
    terms = (cut[:, None] * poly[None]).reshape(3 * nimg, nstamp * STAMP, STAMP)
    design = jnp.concatenate([terms, poly], axis=0)
    both = jnp.einsum(
        "ipx,jpx->ij", design, jnp.concatenate([design, science], axis=0), precision=HI
    )
    gram = both[:, :-1]
    vector = both[:, -1]
    if tiles == 2:
        other = lax.ppermute(both, "tile", [(0, 1), (1, 0)])
        both = both + other
        gram = both[:, :-1]
        vector = both[:, -1]
    else:
        gram, vector = lax.psum((gram, vector), "tile")
    solution = solve_fit(gram, vector)

    difference = subtract_model(solution, images, image, row_coord, col_coord)
    return (difference[None], solution[None])


def solution(mesh):
    return jax.shard_map(
        shards,
        mesh=mesh,
        in_specs=(
            P(("groups", "visit"), "tile", None),
            P("groups", None),
            P("groups", None),
            P(("groups", "visit"), "tile", None, None),
        ),
        out_specs=(P(("groups", "visit"), "tile", None), P(("groups", "visit"), None)),
        check_vma=False,
    )
```

```python
import numpy as np
import jax
import jax.numpy as jnp
from jax import lax
from jax.sharding import PartitionSpec as P
from jax.experimental import pallas as pl
from jax.experimental.pallas import tpu as pltpu

STAMP = 128
KERNEL = 31
HALF = KERNEL // 2
TERMS = 11
SHIFT = 32
LANE = 128
HI = lax.Precision.HIGHEST
CONV = lax.Precision.HIGH


RIDGE = 0.05
SIGMA_LIST = (1.0, 1.0, 1.0, 2.0, 2.0, 4.0)
POWER_LIST = (0, 1, 2, 0, 1, 0)
COLUMN_PICK = (0, 1, 0, 2, 1, 0, 3, 4, 3, 5)
ROW_PICK = (0, 0, 1, 0, 1, 2, 3, 3, 4, 5)


def profile_table():
    taps = np.arange(KERNEL, dtype=np.float64) - HALF
    stacked = []
    for sigma, power in zip(SIGMA_LIST, POWER_LIST):
        bell = np.exp(-taps * taps / (2.0 * sigma * sigma))
        stacked.append(bell * (taps / sigma) ** power / np.sum(bell))
    return np.stack(stacked)


def column_bands(table):
    spans = np.arange(2 * LANE)[:, None] - np.arange(LANE)[None, :]
    inside = (spans >= 0) & (spans < KERNEL)
    picked = table[:, np.clip(spans, 0, KERNEL - 1)]
    return np.where(inside[None], picked, 0.0).astype(np.float32)


def row_bands(table, height):
    spans = np.arange(height + 2 * HALF)[None, :] - np.arange(height)[:, None]
    inside = (spans >= 0) & (spans < KERNEL)
    picked = table[:, np.clip(spans, 0, KERNEL - 1)]
    return np.where(inside[None], picked, 0.0).astype(np.float32)


def coordinates(count, first, total):
    return (
        2.0 * (first + jnp.arange(count, dtype=jnp.int32)).astype(jnp.float32) + 1.0
    ) / total - 1.0


def solve_fit(gram, vector):
    regular = gram + RIDGE * jnp.diag(jnp.diag(gram))
    lower = jnp.linalg.cholesky(regular)
    return jax.scipy.linalg.cho_solve((lower, True), vector)


DIFF_ROWS = 64


def model_kernel(coef_ref, img_ref, exp_ref, row_ref, col_ref, out_ref):
    nimg = img_ref.shape[0]
    ry = row_ref[...]
    cx = col_ref[...]
    flat = coef_ref[3 * nimg] + coef_ref[3 * nimg + 1] * cx + coef_ref[3 * nimg + 2] * ry
    across = jnp.zeros(out_ref.shape, jnp.float32)
    down = jnp.zeros(out_ref.shape, jnp.float32)
    for k in range(nimg):
        plane = img_ref[k]
        flat = flat + coef_ref[3 * k] * plane
        across = across + coef_ref[3 * k + 1] * plane
        down = down + coef_ref[3 * k + 2] * plane
    out_ref[...] = exp_ref[...] - (flat + cx * across + ry * down)


def subtract_model(solution, images, image, row_coord, col_coord):
    nimg, height, width = images.shape
    return pl.pallas_call(
        model_kernel,
        grid=(height // DIFF_ROWS,),
        in_specs=[
            pl.BlockSpec(memory_space=pltpu.SMEM),
            pl.BlockSpec((nimg, DIFF_ROWS, width), lambda i: (0, i, 0)),
            pl.BlockSpec((DIFF_ROWS, width), lambda i: (i, 0)),
            pl.BlockSpec((DIFF_ROWS, 1), lambda i: (i, 0)),
            pl.BlockSpec((1, width), lambda i: (0, 0)),
        ],
        out_specs=pl.BlockSpec((DIFF_ROWS, width), lambda i: (i, 0)),
        out_shape=jax.ShapeDtypeStruct((height, width), jnp.float32),
    )(solution, images, image, row_coord[:, None], col_coord[None, :])


def pick_kernel(rows_ref, blocks_ref, *out_refs):
    for step, out_ref in enumerate(out_refs):
        out_ref[...] = blocks_ref[rows_ref[step]]


def pick_blocks(rows, blocks):
    visits, block, width = blocks.shape
    return pl.pallas_call(
        pick_kernel,
        in_specs=[pl.BlockSpec(memory_space=pltpu.SMEM), pl.BlockSpec(memory_space=pltpu.VMEM)],
        out_shape=[jax.ShapeDtypeStruct((block, width), jnp.float32) for _ in range(visits)],
    )(rows, blocks)


def place_kernel(home_ref, amount_ref, *refs):
    arrived = refs[:-1]
    out_ref = refs[-1]
    block, padded_width = out_ref.shape[1:]
    columns = lax.broadcasted_iota(jnp.int32, (block, padded_width), 1)
    width = arrived[0].shape[1]
    keep = (columns >= HALF) & (columns < HALF + width)
    filler = jnp.zeros((block, padded_width - width), jnp.float32)
    for step, piece in enumerate(arrived):
        wide = jnp.concatenate([piece[...], filler], axis=1)
        turn = (HALF - amount_ref[step] + padded_width) % padded_width
        out_ref[home_ref[step]] = jnp.where(keep, pltpu.roll(wide, turn, 1), 0.0)


def place_blocks(home, amounts, arrived, padded_width):
    visits = len(arrived)
    block = arrived[0].shape[0]
    return pl.pallas_call(
        place_kernel,
        in_specs=[pl.BlockSpec(memory_space=pltpu.SMEM)] * 2
        + [pl.BlockSpec(memory_space=pltpu.VMEM)] * visits,
        out_shape=jax.ShapeDtypeStruct((visits, block, padded_width), jnp.float32),
    )(home, amounts, *arrived)


def shards(exposure, partners, offsets, stamps):
    visits = lax.axis_size("visit")
    tiles = lax.axis_size("tile")
    me = lax.axis_index("visit")
    my_tile = lax.axis_index("tile")
    image = exposure[0]
    height, width = image.shape
    block = height // visits
    chunks = -(-(width + 2 * HALF) // LANE)
    padded_width = chunks * LANE
    table = profile_table()

    blocks = image.reshape(visits, block, width)
    dest_rows = jnp.argmax(partners == me, axis=1).astype(jnp.int32)
    ahead = (me + jnp.arange(visits, dtype=jnp.int32)) % visits
    send_rows = dest_rows[ahead]
    my_sources = (me - jnp.arange(visits, dtype=jnp.int32)) % visits
    home = jnp.argmax(partners[me][None, :] == my_sources[:, None], axis=1).astype(jnp.int32)
    amounts = offsets[me][home].astype(jnp.int32)
    sent = pick_blocks(send_rows, blocks)
    arrived = [sent[0]]
    for step in range(1, visits):
        pairs = [(u, (u + step) % visits) for u in range(visits)]
        arrived.append(lax.ppermute(sent[step], "visit", pairs))
    anchors, arrived[1] = lax.optimization_barrier((stamps[0, 0], arrived[1]))
    placed = place_blocks(home, amounts, arrived, padded_width).reshape(height, padded_width)

    forward = [(i, i + 1) for i in range(tiles - 1)]
    backward = [(i + 1, i) for i in range(tiles - 1)]
    above = lax.ppermute(placed[height - HALF :], "tile", forward)
    below = lax.ppermute(placed[:HALF], "tile", backward)
    field = jnp.concatenate([above, placed, below], axis=0)
    field_rows = height + 2 * HALF

    tiled = field.reshape(field_rows, chunks, LANE)
    windows = jnp.concatenate([tiled[:, : chunks - 1], tiled[:, 1:]], axis=-1)
    col_band = jnp.asarray(column_bands(table))
    filtered = [
        jnp.einsum("ybk,kx->ybx", windows, col_band[f], precision=CONV).reshape(
            field_rows, (chunks - 1) * LANE
        )[:, :width]
        for f in range(len(SIGMA_LIST))
    ]

    chunk_rows = STAMP if height % STAMP == 0 else height
    row_band = row_bands(table, chunk_rows)
    found = {}
    for f in range(len(SIGMA_LIST)):
        terms = [k for k in range(len(COLUMN_PICK)) if COLUMN_PICK[k] == f]
        stacked_band = jnp.asarray(np.concatenate([row_band[ROW_PICK[k]] for k in terms]))
        outs = [
            jnp.dot(
                stacked_band,
                filtered[f][q : q + chunk_rows + 2 * HALF],
                precision=CONV,
            )
            for q in range(0, height, chunk_rows)
        ]
        for slot, k in enumerate(terms):
            found[k] = jnp.concatenate(
                [o[slot * chunk_rows : (slot + 1) * chunk_rows] for o in outs], axis=0
            )
    images = jnp.stack([found[k] for k in range(len(COLUMN_PICK))])
    nimg = images.shape[0]

    row_coord = coordinates(height, my_tile * height, height * tiles)
    col_coord = coordinates(width, 0, width)

    nstamp = anchors.shape[0]
    cuts, science, stamp_rows, stamp_cols = [], [], [], []
    for s in range(nstamp):
        row_start = anchors[s, 0]
        col_start = anchors[s, 1]
        cuts.append(lax.dynamic_slice(images, (0, row_start, col_start), (nimg, STAMP, STAMP)))
        science.append(lax.dynamic_slice(image, (row_start, col_start), (STAMP, STAMP)))
        stamp_rows.append(lax.dynamic_slice_in_dim(row_coord, row_start, STAMP))
        stamp_cols.append(lax.dynamic_slice_in_dim(col_coord, col_start, STAMP))
    cut = jnp.stack(cuts, axis=1).reshape(nimg, nstamp * STAMP, STAMP)
    science = jnp.stack(science).reshape(1, nstamp * STAMP, STAMP)
    ry = jnp.stack(stamp_rows)[:, :, None]
    cx = jnp.stack(stamp_cols)[:, None, :]
    ones = jnp.ones((nstamp, STAMP, STAMP), jnp.float32)
    poly = jnp.stack([ones, ones * cx, ones * ry]).reshape(3, nstamp * STAMP, STAMP)
    terms = (cut[:, None] * poly[None]).reshape(3 * nimg, nstamp * STAMP, STAMP)
    design = jnp.concatenate([terms, poly], axis=0)
    both = jnp.einsum(
        "ipx,jpx->ij", design, jnp.concatenate([design, science], axis=0), precision=HI
    )
    gram = both[:, :-1]
    vector = both[:, -1]
    if tiles == 2:
        other = lax.ppermute(both, "tile", [(0, 1), (1, 0)])
        both = both + other
        gram = both[:, :-1]
        vector = both[:, -1]
    else:
        gram, vector = lax.psum((gram, vector), "tile")
    solution = solve_fit(gram, vector)

    difference = subtract_model(solution, images, image, row_coord, col_coord)
    return (difference[None], solution[None])


def solution(mesh):
    return jax.shard_map(
        shards,
        mesh=mesh,
        in_specs=(
            P(("groups", "visit"), "tile", None),
            P("groups", None),
            P("groups", None),
            P(("groups", "visit"), "tile", None, None),
        ),
        out_specs=(P(("groups", "visit"), "tile", None), P(("groups", "visit"), None)),
        check_vma=False,
    )
```

```python
import numpy as np
import jax
import jax.numpy as jnp
from jax import lax
from jax.sharding import PartitionSpec as P
from jax.experimental import pallas as pl
from jax.experimental.pallas import tpu as pltpu

STAMP = 128
KERNEL = 31
HALF = KERNEL // 2
TERMS = 11
SHIFT = 32
LANE = 128
HI = lax.Precision.HIGHEST
CONV = lax.Precision.HIGH


RIDGE = 0.05
SIGMA_LIST = (1.0, 1.0, 1.0, 2.0, 2.0, 4.0)
POWER_LIST = (0, 1, 2, 0, 1, 0)
COLUMN_PICK = (0, 1, 0, 2, 1, 0, 3, 4, 3, 5)
ROW_PICK = (0, 0, 1, 0, 1, 2, 3, 3, 4, 5)


def profile_table():
    taps = np.arange(KERNEL, dtype=np.float64) - HALF
    stacked = []
    for sigma, power in zip(SIGMA_LIST, POWER_LIST):
        bell = np.exp(-taps * taps / (2.0 * sigma * sigma))
        stacked.append(bell * (taps / sigma) ** power / np.sum(bell))
    return np.stack(stacked)


def column_bands(table):
    spans = np.arange(2 * LANE)[:, None] - np.arange(LANE)[None, :]
    inside = (spans >= 0) & (spans < KERNEL)
    picked = table[:, np.clip(spans, 0, KERNEL - 1)]
    return np.where(inside[None], picked, 0.0).astype(np.float32)


def row_bands(table, height):
    spans = np.arange(height + 2 * HALF)[None, :] - np.arange(height)[:, None]
    inside = (spans >= 0) & (spans < KERNEL)
    picked = table[:, np.clip(spans, 0, KERNEL - 1)]
    return np.where(inside[None], picked, 0.0).astype(np.float32)


def coordinates(count, first, total):
    return (
        2.0 * (first + jnp.arange(count, dtype=jnp.int32)).astype(jnp.float32) + 1.0
    ) / total - 1.0


def solve_fit(gram, vector):
    regular = gram + RIDGE * jnp.diag(jnp.diag(gram))
    lower = jnp.linalg.cholesky(regular)
    return jax.scipy.linalg.cho_solve((lower, True), vector)


DIFF_ROWS = 64


def model_kernel(coef_ref, img_ref, exp_ref, row_ref, col_ref, out_ref):
    nimg = img_ref.shape[0]
    ry = row_ref[...]
    cx = col_ref[...]
    flat = coef_ref[3 * nimg] + coef_ref[3 * nimg + 1] * cx + coef_ref[3 * nimg + 2] * ry
    across = jnp.zeros(out_ref.shape, jnp.float32)
    down = jnp.zeros(out_ref.shape, jnp.float32)
    for k in range(nimg):
        plane = img_ref[k]
        flat = flat + coef_ref[3 * k] * plane
        across = across + coef_ref[3 * k + 1] * plane
        down = down + coef_ref[3 * k + 2] * plane
    out_ref[...] = exp_ref[...] - (flat + cx * across + ry * down)


def subtract_model(solution, images, image, row_coord, col_coord):
    nimg, height, width = images.shape
    return pl.pallas_call(
        model_kernel,
        grid=(height // DIFF_ROWS,),
        in_specs=[
            pl.BlockSpec(memory_space=pltpu.SMEM),
            pl.BlockSpec((nimg, DIFF_ROWS, width), lambda i: (0, i, 0)),
            pl.BlockSpec((DIFF_ROWS, width), lambda i: (i, 0)),
            pl.BlockSpec((DIFF_ROWS, 1), lambda i: (i, 0)),
            pl.BlockSpec((1, width), lambda i: (0, 0)),
        ],
        out_specs=pl.BlockSpec((DIFF_ROWS, width), lambda i: (i, 0)),
        out_shape=jax.ShapeDtypeStruct((height, width), jnp.float32),
    )(solution, images, image, row_coord[:, None], col_coord[None, :])


def pick_kernel(rows_ref, blocks_ref, *out_refs):
    for step, out_ref in enumerate(out_refs):
        out_ref[...] = blocks_ref[rows_ref[step]]


def pick_blocks(rows, blocks):
    visits, block, width = blocks.shape
    return pl.pallas_call(
        pick_kernel,
        in_specs=[pl.BlockSpec(memory_space=pltpu.SMEM), pl.BlockSpec(memory_space=pltpu.VMEM)],
        out_shape=[jax.ShapeDtypeStruct((block, width), jnp.float32) for _ in range(visits)],
    )(rows, blocks)


def place_kernel(home_ref, amount_ref, *refs):
    arrived = refs[:-1]
    out_ref = refs[-1]
    block, padded_width = out_ref.shape[1:]
    columns = lax.broadcasted_iota(jnp.int32, (block, padded_width), 1)
    width = arrived[0].shape[1]
    keep = (columns >= HALF) & (columns < HALF + width)
    filler = jnp.zeros((block, padded_width - width), jnp.float32)
    for step, piece in enumerate(arrived):
        wide = jnp.concatenate([piece[...], filler], axis=1)
        turn = (HALF - amount_ref[step] + padded_width) % padded_width
        out_ref[home_ref[step]] = jnp.where(keep, pltpu.roll(wide, turn, 1), 0.0)


def place_blocks(home, amounts, arrived, padded_width):
    visits = len(arrived)
    block = arrived[0].shape[0]
    return pl.pallas_call(
        place_kernel,
        in_specs=[pl.BlockSpec(memory_space=pltpu.SMEM)] * 2
        + [pl.BlockSpec(memory_space=pltpu.VMEM)] * visits,
        out_shape=jax.ShapeDtypeStruct((visits, block, padded_width), jnp.float32),
    )(home, amounts, *arrived)


def shards(exposure, partners, offsets, stamps):
    visits = lax.axis_size("visit")
    tiles = lax.axis_size("tile")
    me = lax.axis_index("visit")
    my_tile = lax.axis_index("tile")
    image = exposure[0]
    height, width = image.shape
    block = height // visits
    chunks = -(-(width + 2 * HALF) // LANE)
    padded_width = chunks * LANE
    table = profile_table()

    blocks = image.reshape(visits, block, width)
    dest_rows = jnp.argmax(partners == me, axis=1).astype(jnp.int32)
    ahead = (me + jnp.arange(visits, dtype=jnp.int32)) % visits
    send_rows = dest_rows[ahead]
    my_sources = (me - jnp.arange(visits, dtype=jnp.int32)) % visits
    home = jnp.argmax(partners[me][None, :] == my_sources[:, None], axis=1).astype(jnp.int32)
    amounts = offsets[me][home].astype(jnp.int32)
    sent = pick_blocks(send_rows, blocks)
    arrived = [sent[0]]
    for step in range(1, visits):
        pairs = [(u, (u + step) % visits) for u in range(visits)]
        arrived.append(lax.ppermute(sent[step], "visit", pairs))
    placed = place_blocks(home, amounts, arrived, padded_width).reshape(height, padded_width)

    forward = [(i, i + 1) for i in range(tiles - 1)]
    backward = [(i + 1, i) for i in range(tiles - 1)]
    above = lax.ppermute(placed[height - HALF :], "tile", forward)
    below = lax.ppermute(placed[:HALF], "tile", backward)
    field = jnp.concatenate([above, placed, below], axis=0)
    field_rows = height + 2 * HALF

    tiled = field.reshape(field_rows, chunks, LANE)
    windows = jnp.concatenate([tiled[:, : chunks - 1], tiled[:, 1:]], axis=-1)
    col_band = jnp.asarray(column_bands(table))
    filtered = [
        jnp.einsum("ybk,kx->ybx", windows, col_band[f], precision=CONV).reshape(
            field_rows, (chunks - 1) * LANE
        )[:, :width]
        for f in range(len(SIGMA_LIST))
    ]

    chunk_rows = STAMP if height % STAMP == 0 else height
    row_band = row_bands(table, chunk_rows)
    found = {}
    for f in range(len(SIGMA_LIST)):
        terms = [k for k in range(len(COLUMN_PICK)) if COLUMN_PICK[k] == f]
        stacked_band = jnp.asarray(np.concatenate([row_band[ROW_PICK[k]] for k in terms]))
        outs = [
            jnp.dot(
                stacked_band,
                filtered[f][q : q + chunk_rows + 2 * HALF],
                precision=CONV,
            )
            for q in range(0, height, chunk_rows)
        ]
        for slot, k in enumerate(terms):
            found[k] = jnp.concatenate(
                [o[slot * chunk_rows : (slot + 1) * chunk_rows] for o in outs], axis=0
            )
    images = jnp.stack([found[k] for k in range(len(COLUMN_PICK))])
    nimg = images.shape[0]

    row_coord = coordinates(height, my_tile * height, height * tiles)
    col_coord = coordinates(width, 0, width)

    anchors = stamps[0, 0]
    nstamp = anchors.shape[0]
    cuts, science, stamp_rows, stamp_cols = [], [], [], []
    for s in range(nstamp):
        row_start = anchors[s, 0]
        col_start = anchors[s, 1]
        cuts.append(lax.dynamic_slice(images, (0, row_start, col_start), (nimg, STAMP, STAMP)))
        science.append(lax.dynamic_slice(image, (row_start, col_start), (STAMP, STAMP)))
        stamp_rows.append(lax.dynamic_slice_in_dim(row_coord, row_start, STAMP))
        stamp_cols.append(lax.dynamic_slice_in_dim(col_coord, col_start, STAMP))
    cut = jnp.stack(cuts, axis=1).reshape(nimg, nstamp * STAMP, STAMP)
    science = jnp.stack(science).reshape(1, nstamp * STAMP, STAMP)
    ry = jnp.stack(stamp_rows)[:, :, None]
    cx = jnp.stack(stamp_cols)[:, None, :]
    ones = jnp.ones((nstamp, STAMP, STAMP), jnp.float32)
    poly = jnp.stack([ones, ones * cx, ones * ry]).reshape(3, nstamp * STAMP, STAMP)
    terms = (cut[:, None] * poly[None]).reshape(3 * nimg, nstamp * STAMP, STAMP)
    design = jnp.concatenate([terms, poly], axis=0)
    both = jnp.einsum(
        "ipx,jpx->ij", design, jnp.concatenate([design, science], axis=0), precision=CONV
    )
    gram = both[:, :-1]
    vector = both[:, -1]
    if tiles == 2:
        other = lax.ppermute(both, "tile", [(0, 1), (1, 0)])
        both = both + other
        gram = both[:, :-1]
        vector = both[:, -1]
    else:
        gram, vector = lax.psum((gram, vector), "tile")
    solution = solve_fit(gram, vector)

    difference = subtract_model(solution, images, image, row_coord, col_coord)
    return (difference[None], solution[None])


def solution(mesh):
    return jax.shard_map(
        shards,
        mesh=mesh,
        in_specs=(
            P(("groups", "visit"), "tile", None),
            P("groups", None),
            P("groups", None),
            P(("groups", "visit"), "tile", None, None),
        ),
        out_specs=(P(("groups", "visit"), "tile", None), P(("groups", "visit"), None)),
        check_vma=False,
    )
```

```python
import numpy as np
import jax
import jax.numpy as jnp
from jax import lax
from jax.sharding import PartitionSpec as P
from jax.experimental import pallas as pl
from jax.experimental.pallas import tpu as pltpu

STAMP = 128
KERNEL = 31
HALF = KERNEL // 2
TERMS = 11
SHIFT = 32
LANE = 128
HI = lax.Precision.HIGHEST
CONV = lax.Precision.HIGH


RIDGE = 0.05
SIGMA_LIST = (1.0, 1.0, 1.0, 2.0, 2.0, 4.0)
POWER_LIST = (0, 1, 2, 0, 1, 0)
COLUMN_PICK = (0, 1, 0, 2, 1, 0, 3, 4, 3, 5)
ROW_PICK = (0, 0, 1, 0, 1, 2, 3, 3, 4, 5)


def profile_table():
    taps = np.arange(KERNEL, dtype=np.float64) - HALF
    stacked = []
    for sigma, power in zip(SIGMA_LIST, POWER_LIST):
        bell = np.exp(-taps * taps / (2.0 * sigma * sigma))
        stacked.append(bell * (taps / sigma) ** power / np.sum(bell))
    return np.stack(stacked)


def column_bands(table):
    spans = np.arange(2 * LANE)[:, None] - np.arange(LANE)[None, :]
    inside = (spans >= 0) & (spans < KERNEL)
    picked = table[:, np.clip(spans, 0, KERNEL - 1)]
    return np.where(inside[None], picked, 0.0).astype(np.float32)


def row_bands(table, height):
    spans = np.arange(height + 2 * HALF)[None, :] - np.arange(height)[:, None]
    inside = (spans >= 0) & (spans < KERNEL)
    picked = table[:, np.clip(spans, 0, KERNEL - 1)]
    return np.where(inside[None], picked, 0.0).astype(np.float32)


def coordinates(count, first, total):
    return (
        2.0 * (first + jnp.arange(count, dtype=jnp.int32)).astype(jnp.float32) + 1.0
    ) / total - 1.0


def solve_fit(gram, vector):
    regular = gram + RIDGE * jnp.diag(jnp.diag(gram))
    lower = jnp.linalg.cholesky(regular)
    return jax.scipy.linalg.cho_solve((lower, True), vector)


DIFF_ROWS = 64


def model_kernel(coef_ref, img_ref, exp_ref, row_ref, col_ref, out_ref):
    nimg = img_ref.shape[0]
    ry = row_ref[...]
    cx = col_ref[...]
    flat = coef_ref[3 * nimg] + coef_ref[3 * nimg + 1] * cx + coef_ref[3 * nimg + 2] * ry
    across = jnp.zeros(out_ref.shape, jnp.float32)
    down = jnp.zeros(out_ref.shape, jnp.float32)
    for k in range(nimg):
        plane = img_ref[k]
        flat = flat + coef_ref[3 * k] * plane
        across = across + coef_ref[3 * k + 1] * plane
        down = down + coef_ref[3 * k + 2] * plane
    out_ref[...] = exp_ref[...] - (flat + cx * across + ry * down)


def subtract_model(solution, images, image, row_coord, col_coord):
    nimg, height, width = images.shape
    return pl.pallas_call(
        model_kernel,
        grid=(height // DIFF_ROWS,),
        in_specs=[
            pl.BlockSpec(memory_space=pltpu.SMEM),
            pl.BlockSpec((nimg, DIFF_ROWS, width), lambda i: (0, i, 0)),
            pl.BlockSpec((DIFF_ROWS, width), lambda i: (i, 0)),
            pl.BlockSpec((DIFF_ROWS, 1), lambda i: (i, 0)),
            pl.BlockSpec((1, width), lambda i: (0, 0)),
        ],
        out_specs=pl.BlockSpec((DIFF_ROWS, width), lambda i: (i, 0)),
        out_shape=jax.ShapeDtypeStruct((height, width), jnp.float32),
    )(solution, images, image, row_coord[:, None], col_coord[None, :])


def pick_kernel(rows_ref, blocks_ref, *out_refs):
    for step, out_ref in enumerate(out_refs):
        out_ref[...] = blocks_ref[rows_ref[step]]


def pick_blocks(rows, blocks):
    visits, block, width = blocks.shape
    return pl.pallas_call(
        pick_kernel,
        in_specs=[pl.BlockSpec(memory_space=pltpu.SMEM), pl.BlockSpec(memory_space=pltpu.VMEM)],
        out_shape=[jax.ShapeDtypeStruct((block, width), jnp.float32) for _ in range(visits)],
    )(rows, blocks)


def place_kernel(home_ref, amount_ref, *refs):
    arrived = refs[:-1]
    out_ref = refs[-1]
    block, padded_width = out_ref.shape[1:]
    columns = lax.broadcasted_iota(jnp.int32, (block, padded_width), 1)
    width = arrived[0].shape[1]
    keep = (columns >= HALF) & (columns < HALF + width)
    filler = jnp.zeros((block, padded_width - width), jnp.float32)
    for step, piece in enumerate(arrived):
        wide = jnp.concatenate([piece[...], filler], axis=1)
        turn = (HALF - amount_ref[step] + padded_width) % padded_width
        out_ref[home_ref[step]] = jnp.where(keep, pltpu.roll(wide, turn, 1), 0.0)


def place_blocks(home, amounts, arrived, padded_width):
    visits = len(arrived)
    block = arrived[0].shape[0]
    return pl.pallas_call(
        place_kernel,
        in_specs=[pl.BlockSpec(memory_space=pltpu.SMEM)] * 2
        + [pl.BlockSpec(memory_space=pltpu.VMEM)] * visits,
        out_shape=jax.ShapeDtypeStruct((visits, block, padded_width), jnp.float32),
    )(home, amounts, *arrived)


def shards(exposure, partners, offsets, stamps):
    visits = lax.axis_size("visit")
    tiles = lax.axis_size("tile")
    me = lax.axis_index("visit")
    my_tile = lax.axis_index("tile")
    image = exposure[0]
    height, width = image.shape
    block = height // visits
    chunks = -(-(width + 2 * HALF) // LANE)
    padded_width = chunks * LANE
    table = profile_table()

    blocks = image.reshape(visits, block, width)
    dest_rows = jnp.argmax(partners == me, axis=1).astype(jnp.int32)
    ahead = (me + jnp.arange(visits, dtype=jnp.int32)) % visits
    send_rows = dest_rows[ahead]
    my_sources = (me - jnp.arange(visits, dtype=jnp.int32)) % visits
    home = jnp.argmax(partners[me][None, :] == my_sources[:, None], axis=1).astype(jnp.int32)
    amounts = offsets[me][home].astype(jnp.int32)
    sent = pick_blocks(send_rows, blocks)
    arrived = [sent[0]]
    for step in range(1, visits):
        pairs = [(u, (u + step) % visits) for u in range(visits)]
        arrived.append(lax.ppermute(sent[step], "visit", pairs))
    placed = place_blocks(home, amounts, arrived, padded_width).reshape(height, padded_width)

    forward = [(i, i + 1) for i in range(tiles - 1)]
    backward = [(i + 1, i) for i in range(tiles - 1)]
    if tiles == 2:
        edge = jnp.where(my_tile == 0, placed[height - HALF :], placed[:HALF])
        other = lax.ppermute(edge, "tile", [(0, 1), (1, 0)])
        above = jnp.where(my_tile == 1, other, 0.0)
        below = jnp.where(my_tile == 0, other, 0.0)
    else:
        above = lax.ppermute(placed[height - HALF :], "tile", forward)
        below = lax.ppermute(placed[:HALF], "tile", backward)
    field = jnp.concatenate([above, placed, below], axis=0)
    field_rows = height + 2 * HALF

    tiled = field.reshape(field_rows, chunks, LANE)
    windows = jnp.concatenate([tiled[:, : chunks - 1], tiled[:, 1:]], axis=-1)
    col_band = jnp.asarray(column_bands(table))
    filtered = [
        jnp.einsum("ybk,kx->ybx", windows, col_band[f], precision=CONV).reshape(
            field_rows, (chunks - 1) * LANE
        )[:, :width]
        for f in range(len(SIGMA_LIST))
    ]

    chunk_rows = STAMP if height % STAMP == 0 else height
    row_band = row_bands(table, chunk_rows)
    found = {}
    for f in range(len(SIGMA_LIST)):
        terms = [k for k in range(len(COLUMN_PICK)) if COLUMN_PICK[k] == f]
        stacked_band = jnp.asarray(np.concatenate([row_band[ROW_PICK[k]] for k in terms]))
        outs = [
            jnp.dot(
                stacked_band,
                filtered[f][q : q + chunk_rows + 2 * HALF],
                precision=CONV,
            )
            for q in range(0, height, chunk_rows)
        ]
        for slot, k in enumerate(terms):
            found[k] = jnp.concatenate(
                [o[slot * chunk_rows : (slot + 1) * chunk_rows] for o in outs], axis=0
            )
    images = jnp.stack([found[k] for k in range(len(COLUMN_PICK))])
    nimg = images.shape[0]

    row_coord = coordinates(height, my_tile * height, height * tiles)
    col_coord = coordinates(width, 0, width)

    anchors = stamps[0, 0]
    nstamp = anchors.shape[0]
    cuts, science, stamp_rows, stamp_cols = [], [], [], []
    for s in range(nstamp):
        row_start = anchors[s, 0]
        col_start = anchors[s, 1]
        cuts.append(lax.dynamic_slice(images, (0, row_start, col_start), (nimg, STAMP, STAMP)))
        science.append(lax.dynamic_slice(image, (row_start, col_start), (STAMP, STAMP)))
        stamp_rows.append(lax.dynamic_slice_in_dim(row_coord, row_start, STAMP))
        stamp_cols.append(lax.dynamic_slice_in_dim(col_coord, col_start, STAMP))
    cut = jnp.stack(cuts, axis=1).reshape(nimg, nstamp * STAMP, STAMP)
    science = jnp.stack(science).reshape(1, nstamp * STAMP, STAMP)
    ry = jnp.stack(stamp_rows)[:, :, None]
    cx = jnp.stack(stamp_cols)[:, None, :]
    ones = jnp.ones((nstamp, STAMP, STAMP), jnp.float32)
    poly = jnp.stack([ones, ones * cx, ones * ry]).reshape(3, nstamp * STAMP, STAMP)
    terms = (cut[:, None] * poly[None]).reshape(3 * nimg, nstamp * STAMP, STAMP)
    design = jnp.concatenate([terms, poly], axis=0)
    both = jnp.einsum(
        "ipx,jpx->ij", design, jnp.concatenate([design, science], axis=0), precision=CONV
    )
    gram = both[:, :-1]
    vector = both[:, -1]
    if tiles == 2:
        other = lax.ppermute(both, "tile", [(0, 1), (1, 0)])
        both = both + other
        gram = both[:, :-1]
        vector = both[:, -1]
    else:
        gram, vector = lax.psum((gram, vector), "tile")
    solution = solve_fit(gram, vector)

    difference = subtract_model(solution, images, image, row_coord, col_coord)
    return (difference[None], solution[None])


def solution(mesh):
    return jax.shard_map(
        shards,
        mesh=mesh,
        in_specs=(
            P(("groups", "visit"), "tile", None),
            P("groups", None),
            P("groups", None),
            P(("groups", "visit"), "tile", None, None),
        ),
        out_specs=(P(("groups", "visit"), "tile", None), P(("groups", "visit"), None)),
        check_vma=False,
    )
```

```python
import numpy as np
import jax
import jax.numpy as jnp
from jax import lax
from jax.sharding import PartitionSpec as P
from jax.experimental import pallas as pl
from jax.experimental.pallas import tpu as pltpu

STAMP = 128
KERNEL = 31
HALF = KERNEL // 2
TERMS = 11
SHIFT = 32
LANE = 128
HI = lax.Precision.HIGHEST
CONV = lax.Precision.HIGH


RIDGE = 0.05
SIGMA_LIST = (1.0, 1.0, 1.0, 2.0, 2.0, 4.0)
POWER_LIST = (0, 1, 2, 0, 1, 0)
COLUMN_PICK = (0, 1, 0, 2, 1, 0, 3, 4, 3, 5)
ROW_PICK = (0, 0, 1, 0, 1, 2, 3, 3, 4, 5)


def profile_table():
    taps = np.arange(KERNEL, dtype=np.float64) - HALF
    stacked = []
    for sigma, power in zip(SIGMA_LIST, POWER_LIST):
        bell = np.exp(-taps * taps / (2.0 * sigma * sigma))
        stacked.append(bell * (taps / sigma) ** power / np.sum(bell))
    return np.stack(stacked)


def column_bands(table):
    spans = np.arange(2 * LANE)[:, None] - np.arange(LANE)[None, :]
    inside = (spans >= 0) & (spans < KERNEL)
    picked = table[:, np.clip(spans, 0, KERNEL - 1)]
    return np.where(inside[None], picked, 0.0).astype(np.float32)


def row_bands(table, height):
    spans = np.arange(height + 2 * HALF)[None, :] - np.arange(height)[:, None]
    inside = (spans >= 0) & (spans < KERNEL)
    picked = table[:, np.clip(spans, 0, KERNEL - 1)]
    return np.where(inside[None], picked, 0.0).astype(np.float32)


def coordinates(count, first, total):
    return (
        2.0 * (first + jnp.arange(count, dtype=jnp.int32)).astype(jnp.float32) + 1.0
    ) / total - 1.0


def solve_fit(gram, vector):
    regular = gram + RIDGE * jnp.diag(jnp.diag(gram))
    lower = jnp.linalg.cholesky(regular)
    return jax.scipy.linalg.cho_solve((lower, True), vector)


DIFF_ROWS = 128


def model_kernel(coef_ref, img_ref, exp_ref, row_ref, col_ref, out_ref):
    nimg = img_ref.shape[0]
    ry = row_ref[...]
    cx = col_ref[...]
    flat = coef_ref[3 * nimg] + coef_ref[3 * nimg + 1] * cx + coef_ref[3 * nimg + 2] * ry
    across = jnp.zeros(out_ref.shape, jnp.float32)
    down = jnp.zeros(out_ref.shape, jnp.float32)
    for k in range(nimg):
        plane = img_ref[k]
        flat = flat + coef_ref[3 * k] * plane
        across = across + coef_ref[3 * k + 1] * plane
        down = down + coef_ref[3 * k + 2] * plane
    out_ref[...] = exp_ref[...] - (flat + cx * across + ry * down)


def subtract_model(solution, images, image, row_coord, col_coord):
    nimg, height, width = images.shape
    return pl.pallas_call(
        model_kernel,
        grid=(height // DIFF_ROWS,),
        in_specs=[
            pl.BlockSpec(memory_space=pltpu.SMEM),
            pl.BlockSpec((nimg, DIFF_ROWS, width), lambda i: (0, i, 0)),
            pl.BlockSpec((DIFF_ROWS, width), lambda i: (i, 0)),
            pl.BlockSpec((DIFF_ROWS, 1), lambda i: (i, 0)),
            pl.BlockSpec((1, width), lambda i: (0, 0)),
        ],
        out_specs=pl.BlockSpec((DIFF_ROWS, width), lambda i: (i, 0)),
        out_shape=jax.ShapeDtypeStruct((height, width), jnp.float32),
    )(solution, images, image, row_coord[:, None], col_coord[None, :])


def pick_kernel(rows_ref, blocks_ref, *out_refs):
    for step, out_ref in enumerate(out_refs):
        out_ref[...] = blocks_ref[rows_ref[step]]


def pick_blocks(rows, blocks):
    visits, block, width = blocks.shape
    return pl.pallas_call(
        pick_kernel,
        in_specs=[pl.BlockSpec(memory_space=pltpu.SMEM), pl.BlockSpec(memory_space=pltpu.VMEM)],
        out_shape=[jax.ShapeDtypeStruct((block, width), jnp.float32) for _ in range(visits)],
    )(rows, blocks)


def place_kernel(home_ref, amount_ref, *refs):
    arrived = refs[:-1]
    out_ref = refs[-1]
    block, padded_width = out_ref.shape[1:]
    columns = lax.broadcasted_iota(jnp.int32, (block, padded_width), 1)
    width = arrived[0].shape[1]
    keep = (columns >= HALF) & (columns < HALF + width)
    filler = jnp.zeros((block, padded_width - width), jnp.float32)
    for step, piece in enumerate(arrived):
        wide = jnp.concatenate([piece[...], filler], axis=1)
        turn = (HALF - amount_ref[step] + padded_width) % padded_width
        out_ref[home_ref[step]] = jnp.where(keep, pltpu.roll(wide, turn, 1), 0.0)


def place_blocks(home, amounts, arrived, padded_width):
    visits = len(arrived)
    block = arrived[0].shape[0]
    return pl.pallas_call(
        place_kernel,
        in_specs=[pl.BlockSpec(memory_space=pltpu.SMEM)] * 2
        + [pl.BlockSpec(memory_space=pltpu.VMEM)] * visits,
        out_shape=jax.ShapeDtypeStruct((visits, block, padded_width), jnp.float32),
    )(home, amounts, *arrived)


def shards(exposure, partners, offsets, stamps):
    visits = lax.axis_size("visit")
    tiles = lax.axis_size("tile")
    me = lax.axis_index("visit")
    my_tile = lax.axis_index("tile")
    image = exposure[0]
    height, width = image.shape
    block = height // visits
    chunks = -(-(width + 2 * HALF) // LANE)
    padded_width = chunks * LANE
    table = profile_table()

    blocks = image.reshape(visits, block, width)
    dest_rows = jnp.argmax(partners == me, axis=1).astype(jnp.int32)
    ahead = (me + jnp.arange(visits, dtype=jnp.int32)) % visits
    send_rows = dest_rows[ahead]
    my_sources = (me - jnp.arange(visits, dtype=jnp.int32)) % visits
    home = jnp.argmax(partners[me][None, :] == my_sources[:, None], axis=1).astype(jnp.int32)
    amounts = offsets[me][home].astype(jnp.int32)
    sent = pick_blocks(send_rows, blocks)
    arrived = [sent[0]]
    for step in range(1, visits):
        pairs = [(u, (u + step) % visits) for u in range(visits)]
        arrived.append(lax.ppermute(sent[step], "visit", pairs))
    placed = place_blocks(home, amounts, arrived, padded_width).reshape(height, padded_width)

    forward = [(i, i + 1) for i in range(tiles - 1)]
    backward = [(i + 1, i) for i in range(tiles - 1)]
    if tiles == 2:
        edge = jnp.where(my_tile == 0, placed[height - HALF :], placed[:HALF])
        other = lax.ppermute(edge, "tile", [(0, 1), (1, 0)])
        above = jnp.where(my_tile == 1, other, 0.0)
        below = jnp.where(my_tile == 0, other, 0.0)
    else:
        above = lax.ppermute(placed[height - HALF :], "tile", forward)
        below = lax.ppermute(placed[:HALF], "tile", backward)
    field = jnp.concatenate([above, placed, below], axis=0)
    field_rows = height + 2 * HALF

    tiled = field.reshape(field_rows, chunks, LANE)
    windows = jnp.concatenate([tiled[:, : chunks - 1], tiled[:, 1:]], axis=-1)
    col_band = jnp.asarray(column_bands(table))
    filtered = [
        jnp.einsum("ybk,kx->ybx", windows, col_band[f], precision=CONV).reshape(
            field_rows, (chunks - 1) * LANE
        )[:, :width]
        for f in range(len(SIGMA_LIST))
    ]

    chunk_rows = STAMP if height % STAMP == 0 else height
    row_band = row_bands(table, chunk_rows)
    found = {}
    for f in range(len(SIGMA_LIST)):
        terms = [k for k in range(len(COLUMN_PICK)) if COLUMN_PICK[k] == f]
        stacked_band = jnp.asarray(np.concatenate([row_band[ROW_PICK[k]] for k in terms]))
        outs = [
            jnp.dot(
                stacked_band,
                filtered[f][q : q + chunk_rows + 2 * HALF],
                precision=CONV,
            )
            for q in range(0, height, chunk_rows)
        ]
        for slot, k in enumerate(terms):
            found[k] = jnp.concatenate(
                [o[slot * chunk_rows : (slot + 1) * chunk_rows] for o in outs], axis=0
            )
    images = jnp.stack([found[k] for k in range(len(COLUMN_PICK))])
    nimg = images.shape[0]

    row_coord = coordinates(height, my_tile * height, height * tiles)
    col_coord = coordinates(width, 0, width)

    anchors = stamps[0, 0]
    nstamp = anchors.shape[0]
    cuts, science, stamp_rows, stamp_cols = [], [], [], []
    for s in range(nstamp):
        row_start = anchors[s, 0]
        col_start = anchors[s, 1]
        cuts.append(lax.dynamic_slice(images, (0, row_start, col_start), (nimg, STAMP, STAMP)))
        science.append(lax.dynamic_slice(image, (row_start, col_start), (STAMP, STAMP)))
        stamp_rows.append(lax.dynamic_slice_in_dim(row_coord, row_start, STAMP))
        stamp_cols.append(lax.dynamic_slice_in_dim(col_coord, col_start, STAMP))
    cut = jnp.stack(cuts, axis=1).reshape(nimg, nstamp * STAMP, STAMP)
    science = jnp.stack(science).reshape(1, nstamp * STAMP, STAMP)
    ry = jnp.stack(stamp_rows)[:, :, None]
    cx = jnp.stack(stamp_cols)[:, None, :]
    ones = jnp.ones((nstamp, STAMP, STAMP), jnp.float32)
    poly = jnp.stack([ones, ones * cx, ones * ry]).reshape(3, nstamp * STAMP, STAMP)
    terms = (cut[:, None] * poly[None]).reshape(3 * nimg, nstamp * STAMP, STAMP)
    design = jnp.concatenate([terms, poly], axis=0)
    both = jnp.einsum(
        "ipx,jpx->ij", design, jnp.concatenate([design, science], axis=0), precision=CONV
    )
    gram = both[:, :-1]
    vector = both[:, -1]
    if tiles == 2:
        other = lax.ppermute(both, "tile", [(0, 1), (1, 0)])
        both = both + other
        gram = both[:, :-1]
        vector = both[:, -1]
    else:
        gram, vector = lax.psum((gram, vector), "tile")
    solution = solve_fit(gram, vector)

    difference = subtract_model(solution, images, image, row_coord, col_coord)
    return (difference[None], solution[None])


def solution(mesh):
    return jax.shard_map(
        shards,
        mesh=mesh,
        in_specs=(
            P(("groups", "visit"), "tile", None),
            P("groups", None),
            P("groups", None),
            P(("groups", "visit"), "tile", None, None),
        ),
        out_specs=(P(("groups", "visit"), "tile", None), P(("groups", "visit"), None)),
        check_vma=False,
    )
```
